32 devices in a mesh: slab: 4 (over y, core), tile: 8 (over z, x).
Axes of the slice: x: 2, y: 2, z: 4, core: 2. Of those that a mesh axis runs over, the one named last changes fastest.
Arguments:
- a_tiles: float32 [512, 8, 128, 128], P(('slab', 'tile')), may hold values from -0.5 to 0.5
- a_cols: int32 [512, 8], P(('slab', 'tile')), may hold values from 0 to 511, as said below
- p_tiles: float32 [512, 2, 128, 128], P(('slab', 'tile')), may hold values from -1 to 1
- p_cols: int32 [512, 2], P(('slab', 'tile')), may hold values from 0 to 31, as said below
- c_cols: int32 [32, 15], P(('slab', 'tile')), may hold values from 0 to 31, as said below
Outputs:
- galerkin: float32 [32, 15, 128, 128], P(('slab', 'tile'))
The draws below stay inside these ranges and needn't reach their ends.
Inputs may be any that keep to these rules, and one draw needn't show every extreme that they name: `a_cols`: row block g, held by the device at slab s and tile t, names 8 different row blocks: g itself first, the others among the row blocks of its own device, the last 4 row blocks of the device at slab s - 1 and tile t, and the first 4 of the device at slab s + 1 and tile t. `p_cols`: each row names 2 different coarse blocks, owned by devices of its own slab whose tile index is t - 1, t or t + 1 modulo the number of tiles, t being the tile of the row's device. `c_cols`: the row of coarse block r, owned by the device at slab s and tile t, names each coarse block owned by a device at slab s - 1, s or s + 1 and tile t - 2 to t + 2 (both modulo the axis sizes) exactly once, in a drawn order; so every coarse block that the product reaches from row r is stored.
All inputs are finite; a program needn't handle non-finite values.
Results may differ from the reference program's by a relative error of at most 0.0003.
Values sent between devices are 32-bit elements; how exact they have to be, the bound alone decides.
No kernel may reach another device: no remote copies, remote signals or barrier semaphores. Data moves between devices by JAX's collectives and lax.ppermute only.
A program may use at most 192 MiB of HBM per device.

```python
import jax
import jax.numpy as jnp
from jax import lax

BS = 128
RB = 16
KA = 8
KP = 2
CB = 1
RIM = 4
SPREAD = 3
KC = 15
TILES = 8
SLABS = 4
NF = 512
NC = 32
DEVICES = 32


def pick_distinct(key, candidates, valid, count):
    cand_count = candidates.shape[1]
    column_ids = jnp.arange(cand_count, dtype=jnp.int32)
    scores = jax.random.randint(key, candidates.shape, 0, 2 ** 20, dtype=jnp.int32) * cand_count + column_ids[None, :]
    scores = jnp.where(valid, scores, -1 - column_ids[None, :])
    unused, chosen = lax.top_k(scores, count)
    return jnp.take_along_axis(candidates, chosen, axis=1)


def draw_a_cols(key, part):
    row_ids = jnp.arange(NF, dtype=jnp.int32)
    device = row_ids // RB
    within = row_ids % RB
    slab_index = device // TILES
    own_slots = jnp.arange(RB, dtype=jnp.int32)
    rim_slots = jnp.arange(RIM, dtype=jnp.int32)
    own_cand = device[:, None] * RB + own_slots[None, :]
    own_valid = own_slots[None, :] != within[:, None]
    lower_cand = (device[:, None] - TILES) * RB + RB - RIM + rim_slots[None, :]
    lower_valid = jnp.broadcast_to((slab_index >= 1)[:, None], lower_cand.shape)
    upper_cand = (device[:, None] + TILES) * RB + rim_slots[None, :]
    upper_valid = jnp.broadcast_to((slab_index <= SLABS - 2)[:, None], upper_cand.shape)
    candidates = jnp.concatenate([own_cand, lower_cand, upper_cand], axis=1)
    valid = jnp.concatenate([own_valid, lower_valid, upper_valid], axis=1)
    others = pick_distinct(key, candidates, valid, KA - 1)
    return jnp.concatenate([row_ids[:, None], others], axis=1).astype(jnp.int32)


def draw_p_cols(key, part):
    row_ids = jnp.arange(NF, dtype=jnp.int32)
    device = row_ids // RB
    slab_index = device // TILES
    tile_index = device % TILES
    cand_ids = jnp.arange(SPREAD * CB, dtype=jnp.int32)
    step_over = cand_ids // CB - (SPREAD - 1) // 2
    within = cand_ids % CB
    owner_tile = jnp.remainder(tile_index[:, None] + step_over[None, :], TILES)
    candidates = (slab_index[:, None] * TILES + owner_tile) * CB + within[None, :]
    valid = jnp.ones(candidates.shape, dtype=bool)
    return pick_distinct(key, candidates, valid, KP).astype(jnp.int32)


def draw_c_cols(key, part):
    coarse_ids = jnp.arange(NC, dtype=jnp.int32)
    device = coarse_ids // CB
    slab_index = device // TILES
    tile_index = device % TILES
    across = (2 * SPREAD - 1) * CB
    cand_ids = jnp.arange(3 * across, dtype=jnp.int32)
    slab_step = cand_ids // across - 1
    rest = cand_ids % across
    tile_step = rest // CB - (SPREAD - 1)
    within = rest % CB
    cand_slab = jnp.remainder(slab_index[:, None] + slab_step[None, :], SLABS)
    cand_tile = jnp.remainder(tile_index[:, None] + tile_step[None, :], TILES)
    candidates = (cand_slab * TILES + cand_tile) * CB + within[None, :]
    valid = jnp.ones(candidates.shape, dtype=bool)
    return pick_distinct(key, candidates, valid, KC).astype(jnp.int32)


def levels(stream_key, dims, shards, smallest, top_value):
    factor_of = 1.0
    for dim, parts in shards:
        steps = jax.random.uniform(jax.random.fold_in(jax.random.fold_in(stream_key, 6), dim), (parts,), jnp.float32, smallest / len(shards), top_value / len(shards))
        factor_of = factor_of * jnp.repeat(jnp.exp(steps), dims[dim] // parts).reshape((-1,) + (1,) * (len(dims) - 1 - dim))
    return factor_of


def noise(stream_key, extent, spread, reach, pieces=(), kind=jnp.bfloat16):
    drawn = jax.random.normal(stream_key, extent, jnp.float32) * spread
    if len(pieces) > 0:
        drawn = levels(stream_key, extent, pieces, -0.22, 0.18) * drawn
    return jnp.clip(drawn, min=-reach, max=reach).astype(kind)


def setup_inputs(seed: int = 0) -> dict:
    keys = jax.random.split(jax.random.key(seed), 6)
    a_tiles = noise(keys[0], (NF, KA, BS, BS), BS ** -0.5, 0.5, ((0, 32),), jnp.float32)
    a_cols = draw_a_cols(jax.random.fold_in(keys[5], 71), 0)
    p_tiles = noise(keys[2], (NF, KP, BS, BS), (BS // 4) ** -0.5, 1.0, ((0, 32),), jnp.float32)
    p_cols = draw_p_cols(jax.random.fold_in(keys[5], 71), 0)
    c_cols = draw_c_cols(jax.random.fold_in(keys[5], 71), 0)
    return {"a_tiles": a_tiles, "a_cols": a_cols, "p_tiles": p_tiles, "p_cols": p_cols, "c_cols": c_cols}


def reference(a_tiles, a_cols, p_tiles, p_cols, c_cols):
    galerkin = jnp.zeros((NC, KC, BS, BS), jnp.float32)

    def device_step(carry, device):
        first_row = (device * RB).astype(jnp.int32)
        block_a = lax.dynamic_slice_in_dim(a_tiles, first_row, RB, 0)
        cols_a = lax.dynamic_slice_in_dim(a_cols, first_row, RB, 0)
        block_p = lax.dynamic_slice_in_dim(p_tiles, first_row, RB, 0)
        cols_p = lax.dynamic_slice_in_dim(p_cols, first_row, RB, 0)
        picked = p_tiles[cols_a]
        picked_cols = p_cols[cols_a]
        products = jnp.einsum("jaxy,japyz->japxz", block_a, picked, precision=lax.Precision.HIGHEST)
        flat_products = products.reshape(RB, KA * KP, BS, BS)
        flat_keys = picked_cols.reshape(RB, KA * KP)
        wanted = c_cols[cols_p]
        matches = (flat_keys[:, None, None, :] == wanted[:, :, :, None]).astype(jnp.float32)
        grouped = jnp.einsum("jqmn,jnxz->jqmxz", matches, flat_products, precision=lax.Precision.HIGHEST)
        summed = jnp.einsum("jqyx,jqmyz->jqmxz", block_p, grouped, precision=lax.Precision.HIGHEST)
        carry = carry.at[cols_p.reshape(-1)].add(summed.reshape(RB * KP, KC, BS, BS))
        return carry, None

    galerkin, unused = lax.scan(device_step, galerkin, jnp.arange(DEVICES, dtype=jnp.int32))
    return galerkin
```

```python
import functools

import jax
import jax.numpy as jnp
from jax import lax
from jax.experimental import pallas as pl
from jax.experimental.pallas import tpu as pltpu
from jax.sharding import PartitionSpec as P

RIM = 4
HIGHEST = lax.Precision.HIGHEST


def extended(cells, axis, width):
    count = lax.axis_size(axis)
    head = cells[:width]
    tail = cells[cells.shape[0] - width :]
    return jnp.concatenate(
        [
            lax.ppermute(tail, axis, [(i, i + 1) for i in range(count - 1)]),
            cells,
            lax.ppermute(head, axis, [(i + 1, i) for i in range(count - 1)]),
        ],
        axis=0,
    )


def passed_along(value, axis, steps):
    count = lax.axis_size(axis)
    pairs = [(source, (source + steps) % count) for source in range(count)]
    return lax.ppermute(value, axis, pairs)


def triple_kernel(
    coupling_slots, interp_slots, blocks, region, lidx_ref, slot_ref, own_ref, a_ref, ext_ref, out_ref, y_ref
):
    g = pl.program_id(0)
    bs = a_ref.shape[2]

    @pl.when(g == 0)
    def _():
        out_ref[...] = jnp.zeros_like(out_ref)

    y_ref[...] = jnp.zeros_like(y_ref)
    for a in range(coupling_slots):
        row = lidx_ref[g * coupling_slots + a]
        prod = jnp.dot(
            a_ref[0, a], ext_ref[row], precision=HIGHEST, preferred_element_type=jnp.float32
        )
        for p in range(interp_slots):
            slot = slot_ref[(g * coupling_slots + a) * interp_slots + p]
            y_ref[slot] += prod[:, p * bs : (p + 1) * bs]
    pt = ext_ref[RIM + g].T
    owners = [own_ref[g * interp_slots + q] for q in range(interp_slots)]
    for c in range(region):
        res = jnp.dot(pt, y_ref[c], precision=HIGHEST, preferred_element_type=jnp.float32)
        for q in range(interp_slots):
            out_ref[owners[q], c] += res[q * bs : (q + 1) * bs]


def shards(a_tiles, a_cols, p_tiles, p_cols, c_cols):
    rows, coupling_slots, bs, _ = a_tiles.shape
    interp_slots = p_tiles.shape[1]
    blocks, pattern_slots = c_cols.shape
    tiles = lax.axis_size("tile")
    slabs = lax.axis_size("slab")
    t = lax.axis_index("tile")
    s = lax.axis_index("slab")
    device = s * tiles + t
    region = 9 * blocks

    p_cat = p_tiles.transpose(0, 2, 1, 3).reshape(rows, bs, interp_slots * bs)
    ext = extended(p_cat, "slab", RIM)
    ext_keys = extended(p_cols, "slab", RIM)

    own_base = device * rows
    lower_base = (device - tiles) * rows + rows - RIM
    upper_base = (device + tiles) * rows
    local_index = jnp.where(
        a_cols < own_base,
        a_cols - lower_base,
        jnp.where(
            a_cols < own_base + rows,
            RIM + a_cols - own_base,
            RIM + rows + a_cols - upper_base,
        ),
    )
    local_index = jnp.clip(local_index, 0, rows + 2 * RIM - 1)
    keys = ext_keys[local_index]
    k_slab = keys // (tiles * blocks)
    k_tile = (keys // blocks) % tiles
    k_dt = (k_tile - t + 1) % tiles - 1
    slot = ((k_slab - s + 1) * 3 + (k_dt + 1)) * blocks + keys % blocks
    slot = jnp.clip(slot, 0, region - 1)

    targets = p_cols - s * tiles * blocks
    relative = jnp.remainder(targets // blocks - t + 1, tiles)
    owner = jnp.clip(relative * blocks + targets % blocks, 0, 3 * blocks - 1)

    kernel = functools.partial(triple_kernel, coupling_slots, interp_slots, blocks, region)
    out = pl.pallas_call(
        kernel,
        out_shape=jax.ShapeDtypeStruct((3 * blocks, region, bs, bs), jnp.float32),
        grid_spec=pltpu.PrefetchScalarGridSpec(
            num_scalar_prefetch=3,
            grid=(rows,),
            in_specs=[
                pl.BlockSpec((1, coupling_slots, bs, bs), lambda g, *_: (g, 0, 0, 0)),
                pl.BlockSpec(ext.shape, lambda g, *_: (0, 0, 0)),
            ],
            out_specs=pl.BlockSpec((3 * blocks, region, bs, bs), lambda g, *_: (0, 0, 0, 0)),
            scratch_shapes=[pltpu.VMEM((region, bs, bs), jnp.float32)],
        ),
        compiler_params=pltpu.CompilerParams(dimension_semantics=("arbitrary",)),
    )(
        local_index.reshape(-1).astype(jnp.int32),
        slot.reshape(-1).astype(jnp.int32),
        owner.reshape(-1).astype(jnp.int32),
        a_tiles,
        ext,
    )

    own_part = out[blocks : 2 * blocks]
    from_lower = passed_along(out[2 * blocks :], "tile", 1)
    from_upper = passed_along(out[:blocks], "tile", -1)

    c_slab = c_cols // (tiles * blocks)
    c_tile = (c_cols // blocks) % tiles
    c_w = c_cols % blocks
    c_ds = (c_slab - s + 1) % slabs - 1
    c_dt = (c_tile - t + 2) % tiles - 2
    base = (c_ds + 1) * 3
    r_idx = jnp.arange(blocks, dtype=jnp.int32)[:, None]

    def pick(part, dt):
        valid = (dt >= -1) & (dt <= 1)
        idx = jnp.clip((base + dt + 1) * blocks + c_w, 0, region - 1)
        tiles_picked = part[r_idx, idx]
        return jnp.where(valid[:, :, None, None], tiles_picked, 0.0)

    return pick(own_part, c_dt) + pick(from_lower, c_dt + 1) + pick(from_upper, c_dt - 1)


def solution(mesh):
    return jax.shard_map(
        shards,
        mesh=mesh,
        in_specs=(
            P(("slab", "tile"), None, None, None),
            P(("slab", "tile"), None),
            P(("slab", "tile"), None, None, None),
            P(("slab", "tile"), None),
            P(("slab", "tile"), None),
        ),
        out_specs=P(("slab", "tile"), None, None, None),
        check_vma=False,
    )
```

```python
import functools

import jax
import jax.numpy as jnp
from jax import lax
from jax.experimental import pallas as pl
from jax.experimental.pallas import tpu as pltpu
from jax.sharding import PartitionSpec as P

RIM = 4


def extended(cells, axis, width):
    count = lax.axis_size(axis)
    head = cells[:width]
    tail = cells[cells.shape[0] - width :]
    return jnp.concatenate(
        [
            lax.ppermute(tail, axis, [(i, i + 1) for i in range(count - 1)]),
            cells,
            lax.ppermute(head, axis, [(i + 1, i) for i in range(count - 1)]),
        ],
        axis=0,
    )


def passed_along(value, axis, steps):
    count = lax.axis_size(axis)
    pairs = [(source, (source + steps) % count) for source in range(count)]
    return lax.ppermute(value, axis, pairs)


def split(x):
    hi = x.astype(jnp.bfloat16)
    lo = (x - hi.astype(jnp.float32)).astype(jnp.bfloat16)
    return hi, lo


def dot3(x, y):
    xh, xl = x
    yh, yl = y
    f32 = jnp.float32
    return (
        jnp.dot(xh, yh, preferred_element_type=f32)
        + jnp.dot(xh, yl, preferred_element_type=f32)
        + jnp.dot(xl, yh, preferred_element_type=f32)
    )


def triple_kernel(coupling_slots, interp_slots, blocks, region, idx_ref, a_ref, ext_ref, lo_ref, own_ref, hi_ref, y_ref, acc_ref):
    g = pl.program_id(0)
    rows = pl.num_programs(0)
    bs = a_ref.shape[2]
    slot_base = rows * coupling_slots
    owner_base = slot_base + rows * coupling_slots * interp_slots

    @pl.when(g == 0)
    def _():
        acc_ref[...] = jnp.zeros_like(acc_ref)

    y_ref[...] = jnp.zeros_like(y_ref)
    for a in range(coupling_slots):
        row = idx_ref[g * coupling_slots + a]
        prod = dot3(split(a_ref[0, a]), split(ext_ref[row]))
        for p in range(interp_slots):
            slot = idx_ref[slot_base + (g * coupling_slots + a) * interp_slots + p]
            y_ref[slot] += prod[:, p * bs : (p + 1) * bs]
    pt = split(ext_ref[RIM + g].T)
    owners = [idx_ref[owner_base + g * interp_slots + q] for q in range(interp_slots)]
    for c in range(region):
        res = dot3(pt, split(y_ref[c]))
        for q in range(interp_slots):
            acc_ref[owners[q], c] += res[q * bs : (q + 1) * bs]

    @pl.when(g == rows - 1)
    def _():
        lo_ref[...] = acc_ref[:blocks]
        own_ref[...] = acc_ref[blocks : 2 * blocks]
        hi_ref[...] = acc_ref[2 * blocks :]


def shards(a_tiles, a_cols, p_tiles, p_cols, c_cols):
    rows, coupling_slots, bs, _ = a_tiles.shape
    interp_slots = p_tiles.shape[1]
    blocks, pattern_slots = c_cols.shape
    tiles = lax.axis_size("tile")
    slabs = lax.axis_size("slab")
    t = lax.axis_index("tile")
    s = lax.axis_index("slab")
    device = s * tiles + t
    region = 9 * blocks

    p_cat = p_tiles.transpose(0, 2, 1, 3).reshape(rows, bs, interp_slots * bs)
    ext = extended(p_cat, "slab", RIM)
    ext_keys = extended(p_cols, "slab", RIM)

    own_base = device * rows
    lower_base = (device - tiles) * rows + rows - RIM
    upper_base = (device + tiles) * rows
    local_index = jnp.where(
        a_cols < own_base,
        a_cols - lower_base,
        jnp.where(
            a_cols < own_base + rows,
            RIM + a_cols - own_base,
            RIM + rows + a_cols - upper_base,
        ),
    )
    local_index = jnp.clip(local_index, 0, rows + 2 * RIM - 1)
    keys = ext_keys[local_index]
    k_slab = keys // (tiles * blocks)
    k_tile = (keys // blocks) % tiles
    k_dt = (k_tile - t + 1) % tiles - 1
    slot = ((k_slab - s + 1) * 3 + (k_dt + 1)) * blocks + keys % blocks
    slot = jnp.clip(slot, 0, region - 1)

    targets = p_cols - s * tiles * blocks
    relative = jnp.remainder(targets // blocks - t + 1, tiles)
    owner = jnp.clip(relative * blocks + targets % blocks, 0, 3 * blocks - 1)

    kernel = functools.partial(triple_kernel, coupling_slots, interp_slots, blocks, region)
    part = jax.ShapeDtypeStruct((blocks, region, bs, bs), jnp.float32)
    part_spec = pl.BlockSpec((blocks, region, bs, bs), lambda g, *_: (0, 0, 0, 0))
    table = jnp.concatenate(
        [local_index.reshape(-1), slot.reshape(-1), owner.reshape(-1)]
    ).astype(jnp.int32)
    to_lower, own_part, to_upper = pl.pallas_call(
        kernel,
        out_shape=(part, part, part),
        grid_spec=pltpu.PrefetchScalarGridSpec(
            num_scalar_prefetch=1,
            grid=(rows,),
            in_specs=[
                pl.BlockSpec((1, coupling_slots, bs, bs), lambda g, *_: (g, 0, 0, 0)),
                pl.BlockSpec(ext.shape, lambda g, *_: (0, 0, 0)),
            ],
            out_specs=(part_spec, part_spec, part_spec),
            scratch_shapes=[
                pltpu.VMEM((region, bs, bs), jnp.float32),
                pltpu.VMEM((3 * blocks, region, bs, bs), jnp.float32),
            ],
        ),
        compiler_params=pltpu.CompilerParams(dimension_semantics=("arbitrary",)),
    )(table, a_tiles, ext)

    from_lower = passed_along(to_upper, "tile", 1)
    from_upper = passed_along(to_lower, "tile", -1)

    c_slab = c_cols // (tiles * blocks)
    c_tile = (c_cols // blocks) % tiles
    c_w = c_cols % blocks
    c_ds = (c_slab - s + 1) % slabs - 1
    c_dt = (c_tile - t + 2) % tiles - 2
    base = (c_ds + 1) * 3
    r_idx = jnp.arange(blocks, dtype=jnp.int32)[:, None]

    def pick(part, dt):
        valid = (dt >= -1) & (dt <= 1)
        idx = jnp.clip((base + dt + 1) * blocks + c_w, 0, region - 1)
        tiles_picked = part[r_idx, idx]
        return jnp.where(valid[:, :, None, None], tiles_picked, 0.0)

    return pick(own_part, c_dt) + pick(from_lower, c_dt + 1) + pick(from_upper, c_dt - 1)


def solution(mesh):
    return jax.shard_map(
        shards,
        mesh=mesh,
        in_specs=(
            P(("slab", "tile"), None, None, None),
            P(("slab", "tile"), None),
            P(("slab", "tile"), None, None, None),
            P(("slab", "tile"), None),
            P(("slab", "tile"), None),
        ),
        out_specs=P(("slab", "tile"), None, None, None),
        check_vma=False,
    )
```

```python
import functools

import jax
import jax.numpy as jnp
from jax import lax
from jax.experimental import pallas as pl
from jax.experimental.pallas import tpu as pltpu
from jax.sharding import PartitionSpec as P

RIM = 4


def passed_along(value, axis, steps):
    count = lax.axis_size(axis)
    pairs = [(source, (source + steps) % count) for source in range(count)]
    return lax.ppermute(value, axis, pairs)


def split(x):
    hi = x.astype(jnp.bfloat16)
    lo = (x - hi.astype(jnp.float32)).astype(jnp.bfloat16)
    return hi, lo


def dot3(x, y):
    xh, xl = x
    yh, yl = y
    f32 = jnp.float32
    return (
        jnp.dot(xh, yh, preferred_element_type=f32)
        + jnp.dot(xh, yl, preferred_element_type=f32)
        + jnp.dot(xl, yh, preferred_element_type=f32)
    )


def slab_kernel(
    coupling_slots, interp_slots, blocks,
    tbl_ref, a_ref, prow_ref, pown_ref, lo_ref, own_ref, hi_ref,
    y_ref, ph_ref, pl_ref, acc_ref,
):
    g = pl.program_id(0)
    rows = pl.num_programs(0)
    bs = a_ref.shape[2]
    slots = 3 * blocks
    slot_base = rows * coupling_slots
    owner_base = slot_base + rows * coupling_slots * interp_slots
    nz_base = owner_base + rows * interp_slots

    @pl.when(g == 0)
    def _():
        acc_ref[...] = jnp.zeros_like(acc_ref)

        def body(r, carry):
            hi, lo = split(prow_ref[r])
            ph_ref[r] = hi
            pl_ref[r] = lo
            return carry

        lax.fori_loop(0, prow_ref.shape[0], body, 0)

    y_ref[...] = jnp.zeros_like(y_ref)
    for a in range(coupling_slots):
        row = tbl_ref[g * coupling_slots + a]

        @pl.when(row >= 0)
        def _():
            ahl = split(a_ref[0, a])
            j = jnp.maximum(row, 0)
            for p in range(interp_slots):
                prod = dot3(ahl, (ph_ref[j, p], pl_ref[j, p]))
                slot = tbl_ref[slot_base + (g * coupling_slots + a) * interp_slots + p]
                y_ref[slot] += prod

    pt = split(jnp.concatenate([pown_ref[0, q].T for q in range(interp_slots)], axis=0))
    owners = [tbl_ref[owner_base + g * interp_slots + q] for q in range(interp_slots)]
    for c in range(slots):

        @pl.when(tbl_ref[nz_base + g * slots + c] != 0)
        def _():
            res = dot3(pt, split(y_ref[c]))
            for q in range(interp_slots):
                acc_ref[owners[q], c] += res[q * bs : (q + 1) * bs]

    @pl.when(g == rows - 1)
    def _():
        lo_ref[...] = acc_ref[:blocks]
        own_ref[...] = acc_ref[blocks : 2 * blocks]
        hi_ref[...] = acc_ref[2 * blocks :]


def slab_call(table, a_tiles, prow, p_tiles, blocks):
    rows, coupling_slots, bs, _ = a_tiles.shape
    interp_slots = p_tiles.shape[1]
    slots = 3 * blocks
    part = jax.ShapeDtypeStruct((blocks, slots, bs, bs), jnp.float32)
    part_spec = pl.BlockSpec((blocks, slots, bs, bs), lambda g, *_: (0, 0, 0, 0))
    kernel = functools.partial(slab_kernel, coupling_slots, interp_slots, blocks)
    return pl.pallas_call(
        kernel,
        out_shape=(part, part, part),
        grid_spec=pltpu.PrefetchScalarGridSpec(
            num_scalar_prefetch=1,
            grid=(rows,),
            in_specs=[
                pl.BlockSpec((1, coupling_slots, bs, bs), lambda g, *_: (g, 0, 0, 0)),
                pl.BlockSpec(prow.shape, lambda g, *_: (0, 0, 0, 0)),
                pl.BlockSpec((1, interp_slots, bs, bs), lambda g, *_: (g, 0, 0, 0)),
            ],
            out_specs=(part_spec, part_spec, part_spec),
            scratch_shapes=[
                pltpu.VMEM((slots, bs, bs), jnp.float32),
                pltpu.VMEM(prow.shape, jnp.bfloat16),
                pltpu.VMEM(prow.shape, jnp.bfloat16),
                pltpu.VMEM((3 * blocks, slots, bs, bs), jnp.float32),
            ],
        ),
        compiler_params=pltpu.CompilerParams(dimension_semantics=("arbitrary",)),
    )(table, a_tiles, prow, p_tiles)


def shards(a_tiles, a_cols, p_tiles, p_cols, c_cols):
    rows, coupling_slots, bs, _ = a_tiles.shape
    interp_slots = p_tiles.shape[1]
    blocks, pattern_slots = c_cols.shape
    tiles = lax.axis_size("tile")
    slabs = lax.axis_size("slab")
    t = lax.axis_index("tile")
    s = lax.axis_index("slab")
    device = s * tiles + t
    slots = 3 * blocks

    up = [(i, i + 1) for i in range(slabs - 1)]
    down = [(i + 1, i) for i in range(slabs - 1)]
    lower_p, lower_keys = lax.ppermute((p_tiles[rows - RIM :], p_cols[rows - RIM :]), "slab", up)
    upper_p, upper_keys = lax.ppermute((p_tiles[:RIM], p_cols[:RIM]), "slab", down)

    targets = p_cols - s * tiles * blocks
    relative = jnp.remainder(targets // blocks - t + 1, tiles)
    owner = jnp.clip(relative * blocks + targets % blocks, 0, 3 * blocks - 1)

    own_base = device * rows
    lower_base = (device - tiles) * rows + rows - RIM
    upper_base = (device + tiles) * rows
    groups = (
        (a_cols < own_base, a_cols - lower_base, RIM, lower_p, lower_keys),
        ((a_cols >= own_base) & (a_cols < own_base + rows), a_cols - own_base, rows, p_tiles, p_cols),
        (a_cols >= own_base + rows, a_cols - upper_base, RIM, upper_p, upper_keys),
    )
    parts = []
    for inside, local, count, prow, pkeys in groups:
        local = jnp.clip(local, 0, count - 1)
        keys = pkeys[local]
        k_tile = (keys // blocks) % tiles
        slot = ((k_tile - t + 1) % tiles) * blocks + keys % blocks
        slot = jnp.where(inside[:, :, None], jnp.clip(slot, 0, slots - 1), 0)
        hit = inside[:, :, None, None] & (slot[:, :, :, None] == jnp.arange(slots, dtype=jnp.int32))
        nonzero = jnp.any(hit, axis=(1, 2))
        table = jnp.concatenate(
            [
                jnp.where(inside, local, -1).reshape(-1),
                slot.reshape(-1),
                owner.reshape(-1),
                nonzero.astype(jnp.int32).reshape(-1),
            ]
        ).astype(jnp.int32)
        parts.append(slab_call(table, a_tiles, prow, p_tiles, blocks))

    to_lower = [part[0] for part in parts]
    own_part = jnp.concatenate([part[1] for part in parts], axis=1)
    from_lower = jnp.concatenate([passed_along(part[2], "tile", 1) for part in parts], axis=1)
    from_upper = jnp.concatenate([passed_along(x, "tile", -1) for x in to_lower], axis=1)

    region = 9 * blocks
    c_slab = c_cols // (tiles * blocks)
    c_tile = (c_cols // blocks) % tiles
    c_w = c_cols % blocks
    c_ds = (c_slab - s + 1) % slabs - 1
    c_dt = (c_tile - t + 2) % tiles - 2
    base = (c_ds + 1) * 3
    r_idx = jnp.arange(blocks, dtype=jnp.int32)[:, None]

    def pick(part, dt):
        valid = (dt >= -1) & (dt <= 1)
        idx = jnp.clip((base + dt + 1) * blocks + c_w, 0, region - 1)
        tiles_picked = part[r_idx, idx]
        return jnp.where(valid[:, :, None, None], tiles_picked, 0.0)

    return pick(own_part, c_dt) + pick(from_lower, c_dt + 1) + pick(from_upper, c_dt - 1)


def solution(mesh):
    return jax.shard_map(
        shards,
        mesh=mesh,
        in_specs=(
            P(("slab", "tile"), None, None, None),
            P(("slab", "tile"), None),
            P(("slab", "tile"), None, None, None),
            P(("slab", "tile"), None),
            P(("slab", "tile"), None),
        ),
        out_specs=P(("slab", "tile"), None, None, None),
        check_vma=False,
    )
```

```python
import functools

import jax
import jax.numpy as jnp
from jax import lax
from jax.experimental import pallas as pl
from jax.experimental.pallas import tpu as pltpu
from jax.sharding import PartitionSpec as P

RIM = 4


def passed_along(value, axis, steps):
    count = lax.axis_size(axis)
    pairs = [(source, (source + steps) % count) for source in range(count)]
    return lax.ppermute(value, axis, pairs)


def split(x):
    hi = x.astype(jnp.bfloat16)
    lo = (x - hi.astype(jnp.float32)).astype(jnp.bfloat16)
    return hi, lo


def dot3(x, y):
    xh, xl = x
    yh, yl = y
    f32 = jnp.float32
    return (
        jnp.dot(xh, yh, preferred_element_type=f32)
        + jnp.dot(xh, yl, preferred_element_type=f32)
        + jnp.dot(xl, yh, preferred_element_type=f32)
    )


def triple_kernel(
    coupling_slots, interp_slots, blocks, region,
    idx_ref, a_ref, low_ref, mid_ref, up_ref, lo_ref, own_ref, hi_ref,
    y_ref, acc_ref, ph_ref, pl_ref,
):
    g = pl.program_id(0)
    rows = pl.num_programs(0)
    bs = a_ref.shape[2]
    slot_base = rows * coupling_slots
    owner_base = slot_base + rows * coupling_slots * interp_slots

    @pl.when(g == 0)
    def _():
        acc_ref[...] = jnp.zeros_like(acc_ref)

        def fill(src, offset, count):
            def body(r, carry):
                for p in range(interp_slots):
                    hi, lo = split(src[r, p])
                    ph_ref[offset + r, :, p * bs : (p + 1) * bs] = hi
                    pl_ref[offset + r, :, p * bs : (p + 1) * bs] = lo
                return carry

            lax.fori_loop(0, count, body, 0)

        fill(low_ref, 0, RIM)
        fill(mid_ref, RIM, rows)
        fill(up_ref, RIM + rows, RIM)

    y_ref[...] = jnp.zeros_like(y_ref)
    for a in range(coupling_slots):
        row = idx_ref[g * coupling_slots + a]
        prod = dot3(split(a_ref[0, a]), (ph_ref[row], pl_ref[row]))
        for p in range(interp_slots):
            slot = idx_ref[slot_base + (g * coupling_slots + a) * interp_slots + p]
            y_ref[slot] += prod[:, p * bs : (p + 1) * bs]
    pt = split(jnp.concatenate([mid_ref[g, q].T for q in range(interp_slots)], axis=0))
    owners = [idx_ref[owner_base + g * interp_slots + q] for q in range(interp_slots)]
    for c in range(region):
        res = dot3(pt, split(y_ref[c]))
        for q in range(interp_slots):
            acc_ref[owners[q], c] += res[q * bs : (q + 1) * bs]

    @pl.when(g == rows - 1)
    def _():
        lo_ref[...] = acc_ref[:blocks]
        own_ref[...] = acc_ref[blocks : 2 * blocks]
        hi_ref[...] = acc_ref[2 * blocks :]


def shards(a_tiles, a_cols, p_tiles, p_cols, c_cols):
    rows, coupling_slots, bs, _ = a_tiles.shape
    interp_slots = p_tiles.shape[1]
    blocks, pattern_slots = c_cols.shape
    tiles = lax.axis_size("tile")
    slabs = lax.axis_size("slab")
    t = lax.axis_index("tile")
    s = lax.axis_index("slab")
    device = s * tiles + t
    region = 9 * blocks

    ext_rows = rows + 2 * RIM

    def halo(first):
        keys = p_cols[first : first + RIM].astype(jnp.float32).reshape(1, 1, 1, RIM * interp_slots)
        key_tile = jnp.pad(keys, ((0, 0), (0, interp_slots - 1), (0, bs - 1), (0, bs - RIM * interp_slots)))
        return jnp.concatenate([p_tiles[first : first + RIM], key_tile], axis=0)

    low = lax.ppermute(halo(rows - RIM), "slab", [(i, i + 1) for i in range(slabs - 1)])
    up = lax.ppermute(halo(0), "slab", [(i + 1, i) for i in range(slabs - 1)])

    def halo_keys(block):
        return block[RIM, 0, 0, : RIM * interp_slots].astype(jnp.int32).reshape(RIM, interp_slots)

    ext_keys = jnp.concatenate([halo_keys(low), p_cols, halo_keys(up)], axis=0)

    own_base = device * rows
    lower_base = (device - tiles) * rows + rows - RIM
    upper_base = (device + tiles) * rows
    local_index = jnp.where(
        a_cols < own_base,
        a_cols - lower_base,
        jnp.where(
            a_cols < own_base + rows,
            RIM + a_cols - own_base,
            RIM + rows + a_cols - upper_base,
        ),
    )
    local_index = jnp.clip(local_index, 0, ext_rows - 1)
    keys = ext_keys[local_index]
    k_slab = keys // (tiles * blocks)
    k_tile = (keys // blocks) % tiles
    k_dt = (k_tile - t + 1) % tiles - 1
    slot = ((k_slab - s + 1) * 3 + (k_dt + 1)) * blocks + keys % blocks
    slot = jnp.clip(slot, 0, region - 1)

    targets = p_cols - s * tiles * blocks
    relative = jnp.remainder(targets // blocks - t + 1, tiles)
    owner = jnp.clip(relative * blocks + targets % blocks, 0, 3 * blocks - 1)

    kernel = functools.partial(triple_kernel, coupling_slots, interp_slots, blocks, region)
    part = jax.ShapeDtypeStruct((blocks, region, bs, bs), jnp.float32)
    part_spec = pl.BlockSpec((blocks, region, bs, bs), lambda g, *_: (0, 0, 0, 0))
    table = jnp.concatenate(
        [local_index.reshape(-1), slot.reshape(-1), owner.reshape(-1)]
    ).astype(jnp.int32)
    to_lower, own_part, to_upper = pl.pallas_call(
        kernel,
        out_shape=(part, part, part),
        grid_spec=pltpu.PrefetchScalarGridSpec(
            num_scalar_prefetch=1,
            grid=(rows,),
            in_specs=[
                pl.BlockSpec((1, coupling_slots, bs, bs), lambda g, *_: (g, 0, 0, 0)),
                pl.BlockSpec(low.shape, lambda g, *_: (0, 0, 0, 0)),
                pl.BlockSpec(p_tiles.shape, lambda g, *_: (0, 0, 0, 0)),
                pl.BlockSpec(up.shape, lambda g, *_: (0, 0, 0, 0)),
            ],
            out_specs=(part_spec, part_spec, part_spec),
            scratch_shapes=[
                pltpu.VMEM((region, bs, bs), jnp.float32),
                pltpu.VMEM((3 * blocks, region, bs, bs), jnp.float32),
                pltpu.VMEM((ext_rows, bs, interp_slots * bs), jnp.bfloat16),
                pltpu.VMEM((ext_rows, bs, interp_slots * bs), jnp.bfloat16),
            ],
        ),
        compiler_params=pltpu.CompilerParams(dimension_semantics=("arbitrary",)),
    )(table, a_tiles, low, p_tiles, up)

    from_lower = passed_along(to_upper, "tile", 1)
    from_upper = passed_along(to_lower, "tile", -1)

    c_slab = c_cols // (tiles * blocks)
    c_tile = (c_cols // blocks) % tiles
    c_w = c_cols % blocks
    c_ds = (c_slab - s + 1) % slabs - 1
    c_dt = (c_tile - t + 2) % tiles - 2
    base = (c_ds + 1) * 3
    r_idx = jnp.arange(blocks, dtype=jnp.int32)[:, None]

    def pick(part, dt):
        valid = (dt >= -1) & (dt <= 1)
        idx = jnp.clip((base + dt + 1) * blocks + c_w, 0, region - 1)
        tiles_picked = part[r_idx, idx]
        return jnp.where(valid[:, :, None, None], tiles_picked, 0.0)

    return pick(own_part, c_dt) + pick(from_lower, c_dt + 1) + pick(from_upper, c_dt - 1)


def solution(mesh):
    return jax.shard_map(
        shards,
        mesh=mesh,
        in_specs=(
            P(("slab", "tile"), None, None, None),
            P(("slab", "tile"), None),
            P(("slab", "tile"), None, None, None),
            P(("slab", "tile"), None),
            P(("slab", "tile"), None),
        ),
        out_specs=P(("slab", "tile"), None, None, None),
        check_vma=False,
    )
```

```python
import functools

import jax
import jax.numpy as jnp
from jax import lax
from jax.experimental import pallas as pl
from jax.experimental.pallas import tpu as pltpu
from jax.sharding import PartitionSpec as P

RIM = 4


def passed_along(value, axis, steps):
    count = lax.axis_size(axis)
    pairs = [(source, (source + steps) % count) for source in range(count)]
    return lax.ppermute(value, axis, pairs)


def split(x):
    hi = x.astype(jnp.bfloat16)
    lo = (x - hi.astype(jnp.float32)).astype(jnp.bfloat16)
    return hi, lo


def dot3(x, y):
    xh, xl = x
    yh, yl = y
    f32 = jnp.float32
    return (
        jnp.dot(xh, yh, preferred_element_type=f32)
        + jnp.dot(xh, yl, preferred_element_type=f32)
        + jnp.dot(xl, yh, preferred_element_type=f32)
    )


def triple_kernel(
    coupling_slots, interp_slots, blocks, region,
    idx_ref, a_ref, low_ref, mid_ref, up_ref, lo_ref, own_ref, hi_ref,
    y_ref, acc_ref, ph_ref, pl_ref,
):
    g = pl.program_id(0)
    rows = pl.num_programs(0)
    bs = a_ref.shape[2]
    slot_base = rows * coupling_slots
    owner_base = slot_base + rows * coupling_slots * interp_slots

    @pl.when(g == 0)
    def _():
        acc_ref[...] = jnp.zeros_like(acc_ref)

        def fill(src, offset, count):
            def body(r, carry):
                for p in range(interp_slots):
                    hi, lo = split(src[r, p])
                    ph_ref[offset + r, :, p * bs : (p + 1) * bs] = hi
                    pl_ref[offset + r, :, p * bs : (p + 1) * bs] = lo
                return carry

            lax.fori_loop(0, count, body, 0)

        fill(low_ref, 0, RIM)
        fill(mid_ref, RIM, rows)
        fill(up_ref, RIM + rows, RIM)

    y_ref[...] = jnp.zeros_like(y_ref)
    for a in range(coupling_slots):
        row = idx_ref[g * coupling_slots + a]
        prod = dot3(split(a_ref[0, a]), (ph_ref[row], pl_ref[row]))
        for p in range(interp_slots):
            slot = idx_ref[slot_base + (g * coupling_slots + a) * interp_slots + p]
            y_ref[slot] += prod[:, p * bs : (p + 1) * bs]
    pt = split(jnp.concatenate([mid_ref[g, q].T for q in range(interp_slots)], axis=0))
    owners = [idx_ref[owner_base + g * interp_slots + q] for q in range(interp_slots)]
    wide = jnp.concatenate([y_ref[c] for c in range(region)], axis=1)
    res = dot3(pt, split(wide))
    for q in range(interp_slots):
        acc_ref[owners[q]] += res[q * bs : (q + 1) * bs]

    @pl.when(g == rows - 1)
    def _():
        lo_ref[...] = acc_ref[:blocks]
        own_ref[...] = acc_ref[blocks : 2 * blocks]
        hi_ref[...] = acc_ref[2 * blocks :]


def shards(a_tiles, a_cols, p_tiles, p_cols, c_cols):
    rows, coupling_slots, bs, _ = a_tiles.shape
    interp_slots = p_tiles.shape[1]
    blocks, pattern_slots = c_cols.shape
    tiles = lax.axis_size("tile")
    slabs = lax.axis_size("slab")
    t = lax.axis_index("tile")
    s = lax.axis_index("slab")
    device = s * tiles + t
    region = 9 * blocks

    ext_rows = rows + 2 * RIM

    def halo(first):
        keys = p_cols[first : first + RIM].astype(jnp.float32).reshape(1, 1, 1, RIM * interp_slots)
        key_tile = jnp.pad(keys, ((0, 0), (0, interp_slots - 1), (0, bs - 1), (0, bs - RIM * interp_slots)))
        return jnp.concatenate([p_tiles[first : first + RIM], key_tile], axis=0)

    low = lax.ppermute(halo(rows - RIM), "slab", [(i, i + 1) for i in range(slabs - 1)])
    up = lax.ppermute(halo(0), "slab", [(i + 1, i) for i in range(slabs - 1)])

    def halo_keys(block):
        return block[RIM, 0, 0, : RIM * interp_slots].astype(jnp.int32).reshape(RIM, interp_slots)

    ext_keys = jnp.concatenate([halo_keys(low), p_cols, halo_keys(up)], axis=0)

    own_base = device * rows
    lower_base = (device - tiles) * rows + rows - RIM
    upper_base = (device + tiles) * rows
    local_index = jnp.where(
        a_cols < own_base,
        a_cols - lower_base,
        jnp.where(
            a_cols < own_base + rows,
            RIM + a_cols - own_base,
            RIM + rows + a_cols - upper_base,
        ),
    )
    local_index = jnp.clip(local_index, 0, ext_rows - 1)
    keys = ext_keys[local_index]
    k_slab = keys // (tiles * blocks)
    k_tile = (keys // blocks) % tiles
    k_dt = (k_tile - t + 1) % tiles - 1
    slot = ((k_slab - s + 1) * 3 + (k_dt + 1)) * blocks + keys % blocks
    slot = jnp.clip(slot, 0, region - 1)

    targets = p_cols - s * tiles * blocks
    relative = jnp.remainder(targets // blocks - t + 1, tiles)
    owner = jnp.clip(relative * blocks + targets % blocks, 0, 3 * blocks - 1)

    kernel = functools.partial(triple_kernel, coupling_slots, interp_slots, blocks, region)
    part = jax.ShapeDtypeStruct((blocks, bs, region * bs), jnp.float32)
    part_spec = pl.BlockSpec((blocks, bs, region * bs), lambda g, *_: (0, 0, 0))
    table = jnp.concatenate(
        [local_index.reshape(-1), slot.reshape(-1), owner.reshape(-1)]
    ).astype(jnp.int32)
    to_lower, own_part, to_upper = pl.pallas_call(
        kernel,
        out_shape=(part, part, part),
        grid_spec=pltpu.PrefetchScalarGridSpec(
            num_scalar_prefetch=1,
            grid=(rows,),
            in_specs=[
                pl.BlockSpec((1, coupling_slots, bs, bs), lambda g, *_: (g, 0, 0, 0)),
                pl.BlockSpec(low.shape, lambda g, *_: (0, 0, 0, 0)),
                pl.BlockSpec(p_tiles.shape, lambda g, *_: (0, 0, 0, 0)),
                pl.BlockSpec(up.shape, lambda g, *_: (0, 0, 0, 0)),
            ],
            out_specs=(part_spec, part_spec, part_spec),
            scratch_shapes=[
                pltpu.VMEM((region, bs, bs), jnp.float32),
                pltpu.VMEM((3 * blocks, bs, region * bs), jnp.float32),
                pltpu.VMEM((ext_rows, bs, interp_slots * bs), jnp.bfloat16),
                pltpu.VMEM((ext_rows, bs, interp_slots * bs), jnp.bfloat16),
            ],
        ),
        compiler_params=pltpu.CompilerParams(dimension_semantics=("arbitrary",)),
    )(table, a_tiles, low, p_tiles, up)

    def slot_major(part):
        return part.reshape(blocks, bs, region, bs).transpose(0, 2, 1, 3)

    own_part = slot_major(own_part)
    from_lower = slot_major(passed_along(to_upper, "tile", 1))
    from_upper = slot_major(passed_along(to_lower, "tile", -1))

    c_slab = c_cols // (tiles * blocks)
    c_tile = (c_cols // blocks) % tiles
    c_w = c_cols % blocks
    c_ds = (c_slab - s + 1) % slabs - 1
    c_dt = (c_tile - t + 2) % tiles - 2
    base = (c_ds + 1) * 3
    r_idx = jnp.arange(blocks, dtype=jnp.int32)[:, None]

    def pick(part, dt):
        valid = (dt >= -1) & (dt <= 1)
        idx = jnp.clip((base + dt + 1) * blocks + c_w, 0, region - 1)
        tiles_picked = part[r_idx, idx]
        return jnp.where(valid[:, :, None, None], tiles_picked, 0.0)

    return pick(own_part, c_dt) + pick(from_lower, c_dt + 1) + pick(from_upper, c_dt - 1)


def solution(mesh):
    return jax.shard_map(
        shards,
        mesh=mesh,
        in_specs=(
            P(("slab", "tile"), None, None, None),
            P(("slab", "tile"), None),
            P(("slab", "tile"), None, None, None),
            P(("slab", "tile"), None),
            P(("slab", "tile"), None),
        ),
        out_specs=P(("slab", "tile"), None, None, None),
        check_vma=False,
    )
```

```python
import functools

import jax
import jax.numpy as jnp
from jax import lax
from jax.experimental import pallas as pl
from jax.experimental.pallas import tpu as pltpu
from jax.sharding import PartitionSpec as P

RIM = 4


def passed_along(value, axis, steps):
    count = lax.axis_size(axis)
    pairs = [(source, (source + steps) % count) for source in range(count)]
    return lax.ppermute(value, axis, pairs)


def split(x):
    hi = x.astype(jnp.bfloat16)
    lo = (x - hi.astype(jnp.float32)).astype(jnp.bfloat16)
    return hi, lo


def stack_lhs(x):
    hi, lo = split(x)
    return jnp.concatenate([hi, hi, lo], axis=1)


def stack_rhs(y):
    hi, lo = split(y)
    return jnp.concatenate([hi, lo, hi], axis=0)


def triple_kernel(
    coupling_slots, interp_slots, blocks, region,
    idx_ref, a_ref, low_ref, mid_ref, up_ref, lo_ref, own_ref, hi_ref,
    y_ref, acc_ref, p3_ref,
):
    g = pl.program_id(0)
    rows = pl.num_programs(0)
    bs = a_ref.shape[2]
    slot_base = rows * coupling_slots
    owner_base = slot_base + rows * coupling_slots * interp_slots

    @pl.when(g == 0)
    def _():
        acc_ref[...] = jnp.zeros_like(acc_ref)

        def fill(src, offset, count):
            def body(r, carry):
                for p in range(interp_slots):
                    hi, lo = split(src[r, p])
                    cols = slice(p * bs, (p + 1) * bs)
                    p3_ref[offset + r, 0:bs, cols] = hi
                    p3_ref[offset + r, bs : 2 * bs, cols] = lo
                    p3_ref[offset + r, 2 * bs : 3 * bs, cols] = hi
                return carry

            lax.fori_loop(0, count, body, 0)

        fill(low_ref, 0, RIM)
        fill(mid_ref, RIM, rows)
        fill(up_ref, RIM + rows, RIM)

    y_ref[...] = jnp.zeros_like(y_ref)
    for a in range(coupling_slots):
        row = idx_ref[g * coupling_slots + a]
        prod = jnp.dot(stack_lhs(a_ref[0, a]), p3_ref[row], preferred_element_type=jnp.float32)
        for p in range(interp_slots):
            slot = idx_ref[slot_base + (g * coupling_slots + a) * interp_slots + p]
            y_ref[slot] += prod[:, p * bs : (p + 1) * bs]
    pt = stack_lhs(jnp.concatenate([mid_ref[g, q].T for q in range(interp_slots)], axis=0))
    owners = [idx_ref[owner_base + g * interp_slots + q] for q in range(interp_slots)]
    for c in range(region):
        res = jnp.dot(pt, stack_rhs(y_ref[c]), preferred_element_type=jnp.float32)
        for q in range(interp_slots):
            acc_ref[owners[q], c] += res[q * bs : (q + 1) * bs]

    @pl.when(g == rows - 1)
    def _():
        lo_ref[...] = acc_ref[:blocks]
        own_ref[...] = acc_ref[blocks : 2 * blocks]
        hi_ref[...] = acc_ref[2 * blocks :]


def shards(a_tiles, a_cols, p_tiles, p_cols, c_cols):
    rows, coupling_slots, bs, _ = a_tiles.shape
    interp_slots = p_tiles.shape[1]
    blocks, pattern_slots = c_cols.shape
    tiles = lax.axis_size("tile")
    slabs = lax.axis_size("slab")
    t = lax.axis_index("tile")
    s = lax.axis_index("slab")
    device = s * tiles + t
    region = 9 * blocks

    ext_rows = rows + 2 * RIM

    def halo(first):
        keys = p_cols[first : first + RIM].astype(jnp.float32).reshape(1, 1, 1, RIM * interp_slots)
        key_tile = jnp.pad(keys, ((0, 0), (0, interp_slots - 1), (0, bs - 1), (0, bs - RIM * interp_slots)))
        return jnp.concatenate([p_tiles[first : first + RIM], key_tile], axis=0)

    low = lax.ppermute(halo(rows - RIM), "slab", [(i, i + 1) for i in range(slabs - 1)])
    up = lax.ppermute(halo(0), "slab", [(i + 1, i) for i in range(slabs - 1)])

    def halo_keys(block):
        return block[RIM, 0, 0, : RIM * interp_slots].astype(jnp.int32).reshape(RIM, interp_slots)

    ext_keys = jnp.concatenate([halo_keys(low), p_cols, halo_keys(up)], axis=0)

    own_base = device * rows
    lower_base = (device - tiles) * rows + rows - RIM
    upper_base = (device + tiles) * rows
    local_index = jnp.where(
        a_cols < own_base,
        a_cols - lower_base,
        jnp.where(
            a_cols < own_base + rows,
            RIM + a_cols - own_base,
            RIM + rows + a_cols - upper_base,
        ),
    )
    local_index = jnp.clip(local_index, 0, ext_rows - 1)
    keys = ext_keys[local_index]
    k_slab = keys // (tiles * blocks)
    k_tile = (keys // blocks) % tiles
    k_dt = (k_tile - t + 1) % tiles - 1
    slot = ((k_slab - s + 1) * 3 + (k_dt + 1)) * blocks + keys % blocks
    slot = jnp.clip(slot, 0, region - 1)

    targets = p_cols - s * tiles * blocks
    relative = jnp.remainder(targets // blocks - t + 1, tiles)
    owner = jnp.clip(relative * blocks + targets % blocks, 0, 3 * blocks - 1)

    kernel = functools.partial(triple_kernel, coupling_slots, interp_slots, blocks, region)
    part = jax.ShapeDtypeStruct((blocks, region, bs, bs), jnp.float32)
    part_spec = pl.BlockSpec((blocks, region, bs, bs), lambda g, *_: (0, 0, 0, 0))
    table = jnp.concatenate(
        [local_index.reshape(-1), slot.reshape(-1), owner.reshape(-1)]
    ).astype(jnp.int32)
    to_lower, own_part, to_upper = pl.pallas_call(
        kernel,
        out_shape=(part, part, part),
        grid_spec=pltpu.PrefetchScalarGridSpec(
            num_scalar_prefetch=1,
            grid=(rows,),
            in_specs=[
                pl.BlockSpec((1, coupling_slots, bs, bs), lambda g, *_: (g, 0, 0, 0)),
                pl.BlockSpec(low.shape, lambda g, *_: (0, 0, 0, 0)),
                pl.BlockSpec(p_tiles.shape, lambda g, *_: (0, 0, 0, 0)),
                pl.BlockSpec(up.shape, lambda g, *_: (0, 0, 0, 0)),
            ],
            out_specs=(part_spec, part_spec, part_spec),
            scratch_shapes=[
                pltpu.VMEM((region, bs, bs), jnp.float32),
                pltpu.VMEM((3 * blocks, region, bs, bs), jnp.float32),
                pltpu.VMEM((ext_rows, 3 * bs, interp_slots * bs), jnp.bfloat16),
            ],
        ),
        compiler_params=pltpu.CompilerParams(dimension_semantics=("arbitrary",)),
    )(table, a_tiles, low, p_tiles, up)

    from_lower = passed_along(to_upper, "tile", 1)
    from_upper = passed_along(to_lower, "tile", -1)

    c_slab = c_cols // (tiles * blocks)
    c_tile = (c_cols // blocks) % tiles
    c_w = c_cols % blocks
    c_ds = (c_slab - s + 1) % slabs - 1
    c_dt = (c_tile - t + 2) % tiles - 2
    base = (c_ds + 1) * 3
    r_idx = jnp.arange(blocks, dtype=jnp.int32)[:, None]

    def pick(part, dt):
        valid = (dt >= -1) & (dt <= 1)
        idx = jnp.clip((base + dt + 1) * blocks + c_w, 0, region - 1)
        tiles_picked = part[r_idx, idx]
        return jnp.where(valid[:, :, None, None], tiles_picked, 0.0)

    return pick(own_part, c_dt) + pick(from_lower, c_dt + 1) + pick(from_upper, c_dt - 1)


def solution(mesh):
    return jax.shard_map(
        shards,
        mesh=mesh,
        in_specs=(
            P(("slab", "tile"), None, None, None),
            P(("slab", "tile"), None),
            P(("slab", "tile"), None, None, None),
            P(("slab", "tile"), None),
            P(("slab", "tile"), None),
        ),
        out_specs=P(("slab", "tile"), None, None, None),
        check_vma=False,
    )
```

```python
import functools

import jax
import jax.numpy as jnp
from jax import lax
from jax.experimental import pallas as pl
from jax.experimental.pallas import tpu as pltpu
from jax.sharding import PartitionSpec as P

RIM = 4


def passed_along(value, axis, steps):
    count = lax.axis_size(axis)
    pairs = [(source, (source + steps) % count) for source in range(count)]
    return lax.ppermute(value, axis, pairs)


def split(x):
    hi = x.astype(jnp.bfloat16)
    lo = (x - hi.astype(jnp.float32)).astype(jnp.bfloat16)
    return hi, lo


def stack_lhs(x):
    hi, lo = split(x)
    return jnp.concatenate([hi, hi, lo], axis=1)


def stack_rhs(y):
    hi, lo = split(y)
    return jnp.concatenate([hi, lo, hi], axis=0)


def accumulate(idx_ref, owner_base, interp_slots, g, pt, y_tiles, acc_ref):
    bs = pt.shape[1] // 3
    owners = [idx_ref[owner_base + g * interp_slots + q] for q in range(interp_slots)]
    for c, y in enumerate(y_tiles):
        res = jnp.dot(pt, stack_rhs(y), preferred_element_type=jnp.float32)
        for q in range(interp_slots):
            acc_ref[owners[q], c] += res[q * bs : (q + 1) * bs]


def flush(g, rows, blocks, acc_ref, lo_ref, own_ref, hi_ref):
    @pl.when(g == rows - 1)
    def _():
        lo_ref[...] = acc_ref[:blocks]
        own_ref[...] = acc_ref[blocks : 2 * blocks]
        hi_ref[...] = acc_ref[2 * blocks :]


def product_kernel(
    coupling_slots, interp_slots, blocks, group,
    idx_ref, a_ref, low_ref, mid_ref, up_ref, lo_ref, own_ref, hi_ref, rest_ref,
    y_ref, acc_ref, p3_ref,
):
    g = pl.program_id(0)
    rows = pl.num_programs(0)
    bs = a_ref.shape[2]
    slot_base = rows * coupling_slots
    owner_base = slot_base + rows * coupling_slots * interp_slots

    @pl.when(g == 0)
    def _():
        acc_ref[...] = jnp.zeros_like(acc_ref)

        def fill(src, offset, count):
            def body(r, carry):
                for p in range(interp_slots):
                    hi, lo = split(src[r, p])
                    cols = slice(p * bs, (p + 1) * bs)
                    p3_ref[offset + r, 0:bs, cols] = hi
                    p3_ref[offset + r, bs : 2 * bs, cols] = lo
                    p3_ref[offset + r, 2 * bs : 3 * bs, cols] = hi
                return carry

            lax.fori_loop(0, count, body, 0)

        fill(low_ref, 0, RIM)
        fill(mid_ref, RIM, rows)
        fill(up_ref, RIM + rows, RIM)

    y_ref[...] = jnp.zeros_like(y_ref)
    for a in range(coupling_slots):
        row = idx_ref[g * coupling_slots + a]
        prod = jnp.dot(stack_lhs(a_ref[0, a]), p3_ref[row], preferred_element_type=jnp.float32)
        for p in range(interp_slots):
            slot = idx_ref[slot_base + (g * coupling_slots + a) * interp_slots + p]
            y_ref[slot] += prod[:, p * bs : (p + 1) * bs]
    rest_ref[0] = y_ref[group:]
    pt = stack_lhs(jnp.concatenate([mid_ref[g, q].T for q in range(interp_slots)], axis=0))
    accumulate(idx_ref, owner_base, interp_slots, g, pt, [y_ref[c] for c in range(group)], acc_ref)
    flush(g, rows, blocks, acc_ref, lo_ref, own_ref, hi_ref)


def group_kernel(
    coupling_slots, interp_slots, blocks, group,
    idx_ref, y_ref, p_ref, lo_ref, own_ref, hi_ref, acc_ref,
):
    g = pl.program_id(0)
    rows = pl.num_programs(0)
    slot_base = rows * coupling_slots
    owner_base = slot_base + rows * coupling_slots * interp_slots

    @pl.when(g == 0)
    def _():
        acc_ref[...] = jnp.zeros_like(acc_ref)

    pt = stack_lhs(jnp.concatenate([p_ref[0, q].T for q in range(interp_slots)], axis=0))
    accumulate(idx_ref, owner_base, interp_slots, g, pt, [y_ref[0, c] for c in range(group)], acc_ref)
    flush(g, rows, blocks, acc_ref, lo_ref, own_ref, hi_ref)


def shards(a_tiles, a_cols, p_tiles, p_cols, c_cols):
    rows, coupling_slots, bs, _ = a_tiles.shape
    interp_slots = p_tiles.shape[1]
    blocks, pattern_slots = c_cols.shape
    tiles = lax.axis_size("tile")
    slabs = lax.axis_size("slab")
    t = lax.axis_index("tile")
    s = lax.axis_index("slab")
    device = s * tiles + t
    region = 9 * blocks

    ext_rows = rows + 2 * RIM

    def halo(first):
        keys = p_cols[first : first + RIM].astype(jnp.float32).reshape(1, 1, 1, RIM * interp_slots)
        key_tile = jnp.pad(keys, ((0, 0), (0, interp_slots - 1), (0, bs - 1), (0, bs - RIM * interp_slots)))
        return jnp.concatenate([p_tiles[first : first + RIM], key_tile], axis=0)

    low = lax.ppermute(halo(rows - RIM), "slab", [(i, i + 1) for i in range(slabs - 1)])
    up = lax.ppermute(halo(0), "slab", [(i + 1, i) for i in range(slabs - 1)])

    def halo_keys(block):
        return block[RIM, 0, 0, : RIM * interp_slots].astype(jnp.int32).reshape(RIM, interp_slots)

    ext_keys = jnp.concatenate([halo_keys(low), p_cols, halo_keys(up)], axis=0)

    own_base = device * rows
    lower_base = (device - tiles) * rows + rows - RIM
    upper_base = (device + tiles) * rows
    local_index = jnp.where(
        a_cols < own_base,
        a_cols - lower_base,
        jnp.where(
            a_cols < own_base + rows,
            RIM + a_cols - own_base,
            RIM + rows + a_cols - upper_base,
        ),
    )
    local_index = jnp.clip(local_index, 0, ext_rows - 1)
    keys = ext_keys[local_index]
    k_slab = keys // (tiles * blocks)
    k_tile = (keys // blocks) % tiles
    k_dt = (k_tile - t + 1) % tiles - 1
    slot = ((k_slab - s + 1) * 3 + (k_dt + 1)) * blocks + keys % blocks
    slot = jnp.clip(slot, 0, region - 1)

    targets = p_cols - s * tiles * blocks
    relative = jnp.remainder(targets // blocks - t + 1, tiles)
    owner = jnp.clip(relative * blocks + targets % blocks, 0, 3 * blocks - 1)

    group = 3 * blocks
    part = jax.ShapeDtypeStruct((blocks, group, bs, bs), jnp.float32)
    part_spec = pl.BlockSpec((blocks, group, bs, bs), lambda g, *_: (0, 0, 0, 0))
    params = pltpu.CompilerParams(dimension_semantics=("arbitrary",))
    table = jnp.concatenate(
        [local_index.reshape(-1), slot.reshape(-1), owner.reshape(-1)]
    ).astype(jnp.int32)
    *first, rest = pl.pallas_call(
        functools.partial(product_kernel, coupling_slots, interp_slots, blocks, group),
        out_shape=(part, part, part, jax.ShapeDtypeStruct((rows, region - group, bs, bs), jnp.float32)),
        grid_spec=pltpu.PrefetchScalarGridSpec(
            num_scalar_prefetch=1,
            grid=(rows,),
            in_specs=[
                pl.BlockSpec((1, coupling_slots, bs, bs), lambda g, *_: (g, 0, 0, 0)),
                pl.BlockSpec(low.shape, lambda g, *_: (0, 0, 0, 0)),
                pl.BlockSpec(p_tiles.shape, lambda g, *_: (0, 0, 0, 0)),
                pl.BlockSpec(up.shape, lambda g, *_: (0, 0, 0, 0)),
            ],
            out_specs=(
                part_spec, part_spec, part_spec,
                pl.BlockSpec((1, region - group, bs, bs), lambda g, *_: (g, 0, 0, 0)),
            ),
            scratch_shapes=[
                pltpu.VMEM((region, bs, bs), jnp.float32),
                pltpu.VMEM((3 * blocks, group, bs, bs), jnp.float32),
                pltpu.VMEM((ext_rows, 3 * bs, interp_slots * bs), jnp.bfloat16),
            ],
        ),
        compiler_params=params,
        cost_estimate=pl.CostEstimate(
            flops=6 * rows * bs * bs * bs * (coupling_slots * interp_slots + group * interp_slots),
            transcendentals=0,
            bytes_accessed=4 * bs * bs * rows * (coupling_slots + interp_slots + region),
        ),
    )(table, a_tiles, low, p_tiles, up)
    groups = [first]
    received = [(passed_along(first[2], "tile", 1), passed_along(first[0], "tile", -1))]
    for k in range(region // group - 1):
        if k > 0:
            received[-2], rest = lax.optimization_barrier((received[-2], rest))
        groups.append(
            pl.pallas_call(
                functools.partial(group_kernel, coupling_slots, interp_slots, blocks, group),
                out_shape=(part, part, part),
                grid_spec=pltpu.PrefetchScalarGridSpec(
                    num_scalar_prefetch=1,
                    grid=(rows,),
                    in_specs=[
                        pl.BlockSpec((1, group, bs, bs), lambda g, *_, k=k: (g, k, 0, 0)),
                        pl.BlockSpec((1, interp_slots, bs, bs), lambda g, *_: (g, 0, 0, 0)),
                    ],
                    out_specs=(part_spec, part_spec, part_spec),
                    scratch_shapes=[pltpu.VMEM((3 * blocks, group, bs, bs), jnp.float32)],
                ),
                compiler_params=params,
                cost_estimate=pl.CostEstimate(
                    flops=6 * rows * bs * bs * bs * group * interp_slots,
                    transcendentals=0,
                    bytes_accessed=4 * bs * bs * rows * (group + interp_slots),
                ),
            )(table, rest, p_tiles)
        )
        received.append((passed_along(groups[-1][2], "tile", 1), passed_along(groups[-1][0], "tile", -1)))

    own_part = jnp.concatenate([parts[1] for parts in groups], axis=1)
    from_lower = jnp.concatenate([pair[0] for pair in received], axis=1)
    from_upper = jnp.concatenate([pair[1] for pair in received], axis=1)

    c_slab = c_cols // (tiles * blocks)
    c_tile = (c_cols // blocks) % tiles
    c_w = c_cols % blocks
    c_ds = (c_slab - s + 1) % slabs - 1
    c_dt = (c_tile - t + 2) % tiles - 2
    base = (c_ds + 1) * 3
    r_idx = jnp.arange(blocks, dtype=jnp.int32)[:, None]

    def pick(part, dt):
        valid = (dt >= -1) & (dt <= 1)
        idx = jnp.clip((base + dt + 1) * blocks + c_w, 0, region - 1)
        tiles_picked = part[r_idx, idx]
        return jnp.where(valid[:, :, None, None], tiles_picked, 0.0)

    return pick(own_part, c_dt) + pick(from_lower, c_dt + 1) + pick(from_upper, c_dt - 1)


def solution(mesh):
    return jax.shard_map(
        shards,
        mesh=mesh,
        in_specs=(
            P(("slab", "tile"), None, None, None),
            P(("slab", "tile"), None),
            P(("slab", "tile"), None, None, None),
            P(("slab", "tile"), None),
            P(("slab", "tile"), None),
        ),
        out_specs=P(("slab", "tile"), None, None, None),
        check_vma=False,
    )
```

```python
import functools

import jax
import jax.numpy as jnp
from jax import lax
from jax.experimental import pallas as pl
from jax.experimental.pallas import tpu as pltpu
from jax.sharding import PartitionSpec as P

RIM = 4


def passed_along(value, axis, steps):
    count = lax.axis_size(axis)
    pairs = [(source, (source + steps) % count) for source in range(count)]
    return lax.ppermute(value, axis, pairs)


def split(x):
    hi = x.astype(jnp.bfloat16)
    lo = (x - hi.astype(jnp.float32)).astype(jnp.bfloat16)
    return hi, lo


def stack_lhs(x):
    hi, lo = split(x)
    return jnp.concatenate([hi, hi, lo], axis=1)


def stack_rhs(y):
    hi, lo = split(y)
    return jnp.concatenate([hi, lo, hi], axis=0)


def triple_kernel(
    coupling_slots, interp_slots, blocks, region,
    idx_ref, a_ref, low_ref, mid_ref, up_ref, lo_ref, own_ref, hi_ref,
    y_ref, acc_ref, p3_ref,
):
    g = pl.program_id(0)
    steps = pl.num_programs(0)
    per_step = a_ref.shape[0]
    rows = steps * per_step
    bs = a_ref.shape[2]
    slot_base = rows * coupling_slots
    owner_base = slot_base + rows * coupling_slots * interp_slots

    @pl.when(g == 0)
    def _():
        acc_ref[...] = jnp.zeros_like(acc_ref)

        def fill(src, offset, count):
            def body(r, carry):
                for p in range(interp_slots):
                    hi, lo = split(src[r, p])
                    cols = slice(p * bs, (p + 1) * bs)
                    p3_ref[offset + r, 0:bs, cols] = hi
                    p3_ref[offset + r, bs : 2 * bs, cols] = lo
                    p3_ref[offset + r, 2 * bs : 3 * bs, cols] = hi
                return carry

            lax.fori_loop(0, count, body, 0)

        fill(low_ref, 0, RIM)
        fill(mid_ref, RIM, rows)
        fill(up_ref, RIM + rows, RIM)

    def row_step(i, carry):
        gi = g * per_step + i
        y_ref[...] = jnp.zeros_like(y_ref)
        for a in range(coupling_slots):
            row = idx_ref[gi * coupling_slots + a]
            prod = jnp.dot(stack_lhs(a_ref[i, a]), p3_ref[row], preferred_element_type=jnp.float32)
            for p in range(interp_slots):
                slot = idx_ref[slot_base + (gi * coupling_slots + a) * interp_slots + p]
                y_ref[slot] += prod[:, p * bs : (p + 1) * bs]
        pt = stack_lhs(jnp.concatenate([mid_ref[gi, q].T for q in range(interp_slots)], axis=0))
        owners = [idx_ref[owner_base + gi * interp_slots + q] for q in range(interp_slots)]
        for c in range(region):
            res = jnp.dot(pt, stack_rhs(y_ref[c]), preferred_element_type=jnp.float32)
            for q in range(interp_slots):
                acc_ref[owners[q], c] += res[q * bs : (q + 1) * bs]
        return carry

    lax.fori_loop(0, per_step, row_step, 0)

    @pl.when(g == steps - 1)
    def _():
        lo_ref[...] = acc_ref[:blocks]
        own_ref[...] = acc_ref[blocks : 2 * blocks]
        hi_ref[...] = acc_ref[2 * blocks :]


def shards(a_tiles, a_cols, p_tiles, p_cols, c_cols):
    rows, coupling_slots, bs, _ = a_tiles.shape
    interp_slots = p_tiles.shape[1]
    blocks, pattern_slots = c_cols.shape
    tiles = lax.axis_size("tile")
    slabs = lax.axis_size("slab")
    t = lax.axis_index("tile")
    s = lax.axis_index("slab")
    device = s * tiles + t
    region = 9 * blocks

    ext_rows = rows + 2 * RIM

    def halo(first):
        keys = p_cols[first : first + RIM].astype(jnp.float32).reshape(1, 1, 1, RIM * interp_slots)
        key_tile = jnp.pad(keys, ((0, 0), (0, interp_slots - 1), (0, bs - 1), (0, bs - RIM * interp_slots)))
        return jnp.concatenate([p_tiles[first : first + RIM], key_tile], axis=0)

    low = lax.ppermute(halo(rows - RIM), "slab", [(i, i + 1) for i in range(slabs - 1)])
    up = lax.ppermute(halo(0), "slab", [(i + 1, i) for i in range(slabs - 1)])

    def halo_keys(block):
        return block[RIM, 0, 0, : RIM * interp_slots].astype(jnp.int32).reshape(RIM, interp_slots)

    ext_keys = jnp.concatenate([halo_keys(low), p_cols, halo_keys(up)], axis=0)

    own_base = device * rows
    lower_base = (device - tiles) * rows + rows - RIM
    upper_base = (device + tiles) * rows
    local_index = jnp.where(
        a_cols < own_base,
        a_cols - lower_base,
        jnp.where(
            a_cols < own_base + rows,
            RIM + a_cols - own_base,
            RIM + rows + a_cols - upper_base,
        ),
    )
    local_index = jnp.clip(local_index, 0, ext_rows - 1)
    keys = ext_keys[local_index]
    k_slab = keys // (tiles * blocks)
    k_tile = (keys // blocks) % tiles
    k_dt = (k_tile - t + 1) % tiles - 1
    slot = ((k_slab - s + 1) * 3 + (k_dt + 1)) * blocks + keys % blocks
    slot = jnp.clip(slot, 0, region - 1)

    targets = p_cols - s * tiles * blocks
    relative = jnp.remainder(targets // blocks - t + 1, tiles)
    owner = jnp.clip(relative * blocks + targets % blocks, 0, 3 * blocks - 1)

    per_step = next(d for d in (4, 2, 1) if rows % d == 0)
    kernel = functools.partial(triple_kernel, coupling_slots, interp_slots, blocks, region)
    part = jax.ShapeDtypeStruct((blocks, region, bs, bs), jnp.float32)
    part_spec = pl.BlockSpec((blocks, region, bs, bs), lambda g, *_: (0, 0, 0, 0))
    table = jnp.concatenate(
        [local_index.reshape(-1), slot.reshape(-1), owner.reshape(-1)]
    ).astype(jnp.int32)
    to_lower, own_part, to_upper = pl.pallas_call(
        kernel,
        out_shape=(part, part, part),
        grid_spec=pltpu.PrefetchScalarGridSpec(
            num_scalar_prefetch=1,
            grid=(rows // per_step,),
            in_specs=[
                pl.BlockSpec((per_step, coupling_slots, bs, bs), lambda g, *_: (g, 0, 0, 0)),
                pl.BlockSpec(low.shape, lambda g, *_: (0, 0, 0, 0)),
                pl.BlockSpec(p_tiles.shape, lambda g, *_: (0, 0, 0, 0)),
                pl.BlockSpec(up.shape, lambda g, *_: (0, 0, 0, 0)),
            ],
            out_specs=(part_spec, part_spec, part_spec),
            scratch_shapes=[
                pltpu.VMEM((region, bs, bs), jnp.float32),
                pltpu.VMEM((3 * blocks, region, bs, bs), jnp.float32),
                pltpu.VMEM((ext_rows, 3 * bs, interp_slots * bs), jnp.bfloat16),
            ],
        ),
        compiler_params=pltpu.CompilerParams(dimension_semantics=("arbitrary",)),
    )(table, a_tiles, low, p_tiles, up)

    from_lower = passed_along(to_upper, "tile", 1)
    from_upper = passed_along(to_lower, "tile", -1)

    c_slab = c_cols // (tiles * blocks)
    c_tile = (c_cols // blocks) % tiles
    c_w = c_cols % blocks
    c_ds = (c_slab - s + 1) % slabs - 1
    c_dt = (c_tile - t + 2) % tiles - 2
    base = (c_ds + 1) * 3
    r_idx = jnp.arange(blocks, dtype=jnp.int32)[:, None]

    def pick(part, dt):
        valid = (dt >= -1) & (dt <= 1)
        idx = jnp.clip((base + dt + 1) * blocks + c_w, 0, region - 1)
        tiles_picked = part[r_idx, idx]
        return jnp.where(valid[:, :, None, None], tiles_picked, 0.0)

    return pick(own_part, c_dt) + pick(from_lower, c_dt + 1) + pick(from_upper, c_dt - 1)


def solution(mesh):
    return jax.shard_map(
        shards,
        mesh=mesh,
        in_specs=(
            P(("slab", "tile"), None, None, None),
            P(("slab", "tile"), None),
            P(("slab", "tile"), None, None, None),
            P(("slab", "tile"), None),
            P(("slab", "tile"), None),
        ),
        out_specs=P(("slab", "tile"), None, None, None),
        check_vma=False,
    )
```

```python
import functools

import jax
import jax.numpy as jnp
from jax import lax
from jax.experimental import pallas as pl
from jax.experimental.pallas import tpu as pltpu
from jax.sharding import PartitionSpec as P

RIM = 4


def passed_along(value, axis, steps):
    count = lax.axis_size(axis)
    pairs = [(source, (source + steps) % count) for source in range(count)]
    return lax.ppermute(value, axis, pairs)


def split(x):
    hi = x.astype(jnp.bfloat16)
    lo = (x - hi.astype(jnp.float32)).astype(jnp.bfloat16)
    return hi, lo


def stack_lhs(x):
    hi, lo = split(x)
    return jnp.concatenate([hi, hi, lo], axis=1)


def stack_rhs(y):
    hi, lo = split(y)
    return jnp.concatenate([hi, lo, hi], axis=0)


def triple_kernel(
    coupling_slots, interp_slots, blocks, region,
    idx_ref, a_ref, low_ref, mid_ref, up_ref, lo_ref, own_ref, hi_ref,
    y_ref, acc_ref, pt3_ref, p3_ref,
):
    g = pl.program_id(0)
    steps = pl.num_programs(0)
    per_step = a_ref.shape[0]
    rows = steps * per_step
    bs = a_ref.shape[2]
    slot_base = rows * coupling_slots
    owner_base = slot_base + rows * coupling_slots * interp_slots

    @pl.when(g == 0)
    def _():
        acc_ref[...] = jnp.zeros_like(acc_ref)

        def fill(src, offset, count, stage_two):
            def body(r, carry):
                for p in range(interp_slots):
                    rows_p = slice(p * bs, (p + 1) * bs)
                    th, tl = split(src[r, p].T)
                    pt3_ref[offset + r, rows_p, 0:bs] = th
                    pt3_ref[offset + r, rows_p, bs : 2 * bs] = th
                    pt3_ref[offset + r, rows_p, 2 * bs : 3 * bs] = tl
                    if stage_two:
                        hi, lo = split(src[r, p])
                        p3_ref[r, 0:bs, rows_p] = hi
                        p3_ref[r, bs : 2 * bs, rows_p] = lo
                        p3_ref[r, 2 * bs : 3 * bs, rows_p] = hi
                return carry

            lax.fori_loop(0, count, body, 0)

        fill(low_ref, 0, RIM, False)
        fill(mid_ref, RIM, rows, True)
        fill(up_ref, RIM + rows, RIM, False)

    def row_step(i, carry):
        gi = g * per_step + i
        y_ref[...] = jnp.zeros_like(y_ref)
        for a in range(coupling_slots):
            row = idx_ref[gi * coupling_slots + a]
            ah, al = split(a_ref[i, a])
            a3 = jnp.concatenate([ah, al, ah], axis=1)
            prod_t = lax.dot_general(
                pt3_ref[row], a3, (((1,), (1,)), ((), ())), preferred_element_type=jnp.float32
            )
            for p in range(interp_slots):
                slot = idx_ref[slot_base + (gi * coupling_slots + a) * interp_slots + p]
                y_ref[slot] += prod_t[p * bs : (p + 1) * bs]
        owners = [idx_ref[owner_base + gi * interp_slots + q] for q in range(interp_slots)]
        pieces = []
        for c in range(region):
            yh, yl = split(y_ref[c])
            pieces.append(jnp.concatenate([yh, yh, yl], axis=1))
        res = jnp.dot(jnp.concatenate(pieces, axis=0), p3_ref[gi], preferred_element_type=jnp.float32)
        for c in range(region):
            for q in range(interp_slots):
                acc_ref[owners[q], c] += res[c * bs : (c + 1) * bs, q * bs : (q + 1) * bs]
        return carry

    lax.fori_loop(0, per_step, row_step, 0)

    @pl.when(g == steps - 1)
    def _():
        for o, out in enumerate((lo_ref, own_ref, hi_ref)):
            for w in range(blocks):
                for c in range(region):
                    out[w, c] = acc_ref[o * blocks + w, c].T


def shards(a_tiles, a_cols, p_tiles, p_cols, c_cols):
    rows, coupling_slots, bs, _ = a_tiles.shape
    interp_slots = p_tiles.shape[1]
    blocks, pattern_slots = c_cols.shape
    tiles = lax.axis_size("tile")
    slabs = lax.axis_size("slab")
    t = lax.axis_index("tile")
    s = lax.axis_index("slab")
    device = s * tiles + t
    region = 9 * blocks

    ext_rows = rows + 2 * RIM

    def halo(first):
        keys = p_cols[first : first + RIM].astype(jnp.float32).reshape(1, 1, 1, RIM * interp_slots)
        key_tile = jnp.pad(keys, ((0, 0), (0, interp_slots - 1), (0, bs - 1), (0, bs - RIM * interp_slots)))
        return jnp.concatenate([p_tiles[first : first + RIM], key_tile], axis=0)

    low = lax.ppermute(halo(rows - RIM), "slab", [(i, i + 1) for i in range(slabs - 1)])
    up = lax.ppermute(halo(0), "slab", [(i + 1, i) for i in range(slabs - 1)])

    def halo_keys(block):
        return block[RIM, 0, 0, : RIM * interp_slots].astype(jnp.int32).reshape(RIM, interp_slots)

    ext_keys = jnp.concatenate([halo_keys(low), p_cols, halo_keys(up)], axis=0)

    own_base = device * rows
    lower_base = (device - tiles) * rows + rows - RIM
    upper_base = (device + tiles) * rows
    local_index = jnp.where(
        a_cols < own_base,
        a_cols - lower_base,
        jnp.where(
            a_cols < own_base + rows,
            RIM + a_cols - own_base,
            RIM + rows + a_cols - upper_base,
        ),
    )
    local_index = jnp.clip(local_index, 0, ext_rows - 1)
    keys = ext_keys[local_index]
    k_slab = keys // (tiles * blocks)
    k_tile = (keys // blocks) % tiles
    k_dt = (k_tile - t + 1) % tiles - 1
    slot = ((k_slab - s + 1) * 3 + (k_dt + 1)) * blocks + keys % blocks
    slot = jnp.clip(slot, 0, region - 1)

    targets = p_cols - s * tiles * blocks
    relative = jnp.remainder(targets // blocks - t + 1, tiles)
    owner = jnp.clip(relative * blocks + targets % blocks, 0, 3 * blocks - 1)

    per_step = next(d for d in (4, 2, 1) if rows % d == 0)
    kernel = functools.partial(triple_kernel, coupling_slots, interp_slots, blocks, region)
    part = jax.ShapeDtypeStruct((blocks, region, bs, bs), jnp.float32)
    part_spec = pl.BlockSpec((blocks, region, bs, bs), lambda g, *_: (0, 0, 0, 0))
    table = jnp.concatenate(
        [local_index.reshape(-1), slot.reshape(-1), owner.reshape(-1)]
    ).astype(jnp.int32)
    to_lower, own_part, to_upper = pl.pallas_call(
        kernel,
        out_shape=(part, part, part),
        grid_spec=pltpu.PrefetchScalarGridSpec(
            num_scalar_prefetch=1,
            grid=(rows // per_step,),
            in_specs=[
                pl.BlockSpec((per_step, coupling_slots, bs, bs), lambda g, *_: (g, 0, 0, 0)),
                pl.BlockSpec(low.shape, lambda g, *_: (0, 0, 0, 0)),
                pl.BlockSpec(p_tiles.shape, lambda g, *_: (0, 0, 0, 0)),
                pl.BlockSpec(up.shape, lambda g, *_: (0, 0, 0, 0)),
            ],
            out_specs=(part_spec, part_spec, part_spec),
            scratch_shapes=[
                pltpu.VMEM((region, bs, bs), jnp.float32),
                pltpu.VMEM((3 * blocks, region, bs, bs), jnp.float32),
                pltpu.VMEM((ext_rows, interp_slots * bs, 3 * bs), jnp.bfloat16),
                pltpu.VMEM((rows, 3 * bs, interp_slots * bs), jnp.bfloat16),
            ],
        ),
        compiler_params=pltpu.CompilerParams(dimension_semantics=("arbitrary",)),
    )(table, a_tiles, low, p_tiles, up)

    from_lower = passed_along(to_upper, "tile", 1)
    from_upper = passed_along(to_lower, "tile", -1)

    c_slab = c_cols // (tiles * blocks)
    c_tile = (c_cols // blocks) % tiles
    c_w = c_cols % blocks
    c_ds = (c_slab - s + 1) % slabs - 1
    c_dt = (c_tile - t + 2) % tiles - 2
    base = (c_ds + 1) * 3
    r_idx = jnp.arange(blocks, dtype=jnp.int32)[:, None]

    def pick(part, dt):
        valid = (dt >= -1) & (dt <= 1)
        idx = jnp.clip((base + dt + 1) * blocks + c_w, 0, region - 1)
        tiles_picked = part[r_idx, idx]
        return jnp.where(valid[:, :, None, None], tiles_picked, 0.0)

    return pick(own_part, c_dt) + pick(from_lower, c_dt + 1) + pick(from_upper, c_dt - 1)


def solution(mesh):
    return jax.shard_map(
        shards,
        mesh=mesh,
        in_specs=(
            P(("slab", "tile"), None, None, None),
            P(("slab", "tile"), None),
            P(("slab", "tile"), None, None, None),
            P(("slab", "tile"), None),
            P(("slab", "tile"), None),
        ),
        out_specs=P(("slab", "tile"), None, None, None),
        check_vma=False,
    )
```

```python
import functools

import jax
import jax.numpy as jnp
from jax import lax
from jax.experimental import pallas as pl
from jax.experimental.pallas import tpu as pltpu
from jax.sharding import PartitionSpec as P

RIM = 4


def passed_along(value, axis, steps):
    count = lax.axis_size(axis)
    pairs = [(source, (source + steps) % count) for source in range(count)]
    return lax.ppermute(value, axis, pairs)


def split(x):
    hi = x.astype(jnp.bfloat16)
    lo = (x - hi.astype(jnp.float32)).astype(jnp.bfloat16)
    return hi, lo


def stack_lhs(x):
    hi, lo = split(x)
    return jnp.concatenate([hi, hi, lo], axis=1)


def stack_rhs(y):
    hi, lo = split(y)
    return jnp.concatenate([hi, lo, hi], axis=0)


def triple_kernel(
    coupling_slots, interp_slots, blocks, region,
    idx_ref, a_ref, al_ref, low_ref, mid_ref, up_ref, lo_ref, own_ref, hi_ref,
    y_ref, acc_ref, p3_ref,
):
    g = pl.program_id(0)
    steps = pl.num_programs(0)
    per_step = a_ref.shape[0]
    rows = steps * per_step
    bs = a_ref.shape[2]
    slot_base = rows * coupling_slots
    owner_base = slot_base + rows * coupling_slots * interp_slots

    @pl.when(g == 0)
    def _():
        acc_ref[...] = jnp.zeros_like(acc_ref)

        def fill(src, offset, count):
            def body(r, carry):
                for p in range(interp_slots):
                    hi, lo = split(src[r, p])
                    cols = slice(p * bs, (p + 1) * bs)
                    p3_ref[offset + r, 0:bs, cols] = hi
                    p3_ref[offset + r, bs : 2 * bs, cols] = lo
                    p3_ref[offset + r, 2 * bs : 3 * bs, cols] = hi
                return carry

            lax.fori_loop(0, count, body, 0)

        fill(low_ref, 0, RIM)
        fill(mid_ref, RIM, rows)
        fill(up_ref, RIM + rows, RIM)

    def row_step(i, carry):
        gi = g * per_step + i
        y_ref[...] = jnp.zeros_like(y_ref)
        for a in range(coupling_slots):
            row = idx_ref[gi * coupling_slots + a]
            ah = a_ref[i, a]
            lhs = jnp.concatenate([ah, ah, al_ref[i, a]], axis=1)
            prod = jnp.dot(lhs, p3_ref[row], preferred_element_type=jnp.float32)
            for p in range(interp_slots):
                slot = idx_ref[slot_base + (gi * coupling_slots + a) * interp_slots + p]
                y_ref[slot] += prod[:, p * bs : (p + 1) * bs]
        pt = stack_lhs(jnp.concatenate([mid_ref[gi, q].T for q in range(interp_slots)], axis=0))
        owners = [idx_ref[owner_base + gi * interp_slots + q] for q in range(interp_slots)]
        for c in range(region):
            res = jnp.dot(pt, stack_rhs(y_ref[c]), preferred_element_type=jnp.float32)
            for q in range(interp_slots):
                acc_ref[owners[q], c] += res[q * bs : (q + 1) * bs]
        return carry

    lax.fori_loop(0, per_step, row_step, 0)

    @pl.when(g == steps - 1)
    def _():
        lo_ref[...] = acc_ref[:blocks]
        own_ref[...] = acc_ref[blocks : 2 * blocks]
        hi_ref[...] = acc_ref[2 * blocks :]


def shards(a_tiles, a_cols, p_tiles, p_cols, c_cols):
    rows, coupling_slots, bs, _ = a_tiles.shape
    interp_slots = p_tiles.shape[1]
    blocks, pattern_slots = c_cols.shape
    tiles = lax.axis_size("tile")
    slabs = lax.axis_size("slab")
    t = lax.axis_index("tile")
    s = lax.axis_index("slab")
    device = s * tiles + t
    region = 9 * blocks

    ext_rows = rows + 2 * RIM

    def halo(first):
        keys = p_cols[first : first + RIM].astype(jnp.float32).reshape(1, 1, 1, RIM * interp_slots)
        key_tile = jnp.pad(keys, ((0, 0), (0, interp_slots - 1), (0, bs - 1), (0, bs - RIM * interp_slots)))
        return jnp.concatenate([p_tiles[first : first + RIM], key_tile], axis=0)

    low = lax.ppermute(halo(rows - RIM), "slab", [(i, i + 1) for i in range(slabs - 1)])
    up = lax.ppermute(halo(0), "slab", [(i + 1, i) for i in range(slabs - 1)])

    def halo_keys(block):
        return block[RIM, 0, 0, : RIM * interp_slots].astype(jnp.int32).reshape(RIM, interp_slots)

    ext_keys = jnp.concatenate([halo_keys(low), p_cols, halo_keys(up)], axis=0)

    own_base = device * rows
    lower_base = (device - tiles) * rows + rows - RIM
    upper_base = (device + tiles) * rows
    local_index = jnp.where(
        a_cols < own_base,
        a_cols - lower_base,
        jnp.where(
            a_cols < own_base + rows,
            RIM + a_cols - own_base,
            RIM + rows + a_cols - upper_base,
        ),
    )
    local_index = jnp.clip(local_index, 0, ext_rows - 1)
    keys = ext_keys[local_index]
    k_slab = keys // (tiles * blocks)
    k_tile = (keys // blocks) % tiles
    k_dt = (k_tile - t + 1) % tiles - 1
    slot = ((k_slab - s + 1) * 3 + (k_dt + 1)) * blocks + keys % blocks
    slot = jnp.clip(slot, 0, region - 1)

    targets = p_cols - s * tiles * blocks
    relative = jnp.remainder(targets // blocks - t + 1, tiles)
    owner = jnp.clip(relative * blocks + targets % blocks, 0, 3 * blocks - 1)

    per_step = next(d for d in (4, 2, 1) if rows % d == 0)
    a_round = lax.reduce_precision(a_tiles, exponent_bits=8, mantissa_bits=7)
    a_hi = a_round.astype(jnp.bfloat16)
    a_lo = (a_tiles - a_round).astype(jnp.bfloat16)
    kernel = functools.partial(triple_kernel, coupling_slots, interp_slots, blocks, region)
    part = jax.ShapeDtypeStruct((blocks, region, bs, bs), jnp.float32)
    part_spec = pl.BlockSpec((blocks, region, bs, bs), lambda g, *_: (0, 0, 0, 0))
    table = jnp.concatenate(
        [local_index.reshape(-1), slot.reshape(-1), owner.reshape(-1)]
    ).astype(jnp.int32)
    to_lower, own_part, to_upper = pl.pallas_call(
        kernel,
        out_shape=(part, part, part),
        grid_spec=pltpu.PrefetchScalarGridSpec(
            num_scalar_prefetch=1,
            grid=(rows // per_step,),
            in_specs=[
                pl.BlockSpec((per_step, coupling_slots, bs, bs), lambda g, *_: (g, 0, 0, 0)),
                pl.BlockSpec((per_step, coupling_slots, bs, bs), lambda g, *_: (g, 0, 0, 0)),
                pl.BlockSpec(low.shape, lambda g, *_: (0, 0, 0, 0)),
                pl.BlockSpec(p_tiles.shape, lambda g, *_: (0, 0, 0, 0)),
                pl.BlockSpec(up.shape, lambda g, *_: (0, 0, 0, 0)),
            ],
            out_specs=(part_spec, part_spec, part_spec),
            scratch_shapes=[
                pltpu.VMEM((region, bs, bs), jnp.float32),
                pltpu.VMEM((3 * blocks, region, bs, bs), jnp.float32),
                pltpu.VMEM((ext_rows, 3 * bs, interp_slots * bs), jnp.bfloat16),
            ],
        ),
        compiler_params=pltpu.CompilerParams(dimension_semantics=("arbitrary",)),
    )(table, a_hi, a_lo, low, p_tiles, up)

    from_lower = passed_along(to_upper, "tile", 1)
    from_upper = passed_along(to_lower, "tile", -1)

    c_slab = c_cols // (tiles * blocks)
    c_tile = (c_cols // blocks) % tiles
    c_w = c_cols % blocks
    c_ds = (c_slab - s + 1) % slabs - 1
    c_dt = (c_tile - t + 2) % tiles - 2
    base = (c_ds + 1) * 3
    r_idx = jnp.arange(blocks, dtype=jnp.int32)[:, None]

    def pick(part, dt):
        valid = (dt >= -1) & (dt <= 1)
        idx = jnp.clip((base + dt + 1) * blocks + c_w, 0, region - 1)
        tiles_picked = part[r_idx, idx]
        return jnp.where(valid[:, :, None, None], tiles_picked, 0.0)

    return pick(own_part, c_dt) + pick(from_lower, c_dt + 1) + pick(from_upper, c_dt - 1)


def solution(mesh):
    return jax.shard_map(
        shards,
        mesh=mesh,
        in_specs=(
            P(("slab", "tile"), None, None, None),
            P(("slab", "tile"), None),
            P(("slab", "tile"), None, None, None),
            P(("slab", "tile"), None),
            P(("slab", "tile"), None),
        ),
        out_specs=P(("slab", "tile"), None, None, None),
        check_vma=False,
    )
```

```python
import functools

import jax
import jax.numpy as jnp
from jax import lax
from jax.experimental import pallas as pl
from jax.experimental.pallas import tpu as pltpu
from jax.sharding import PartitionSpec as P

RIM = 4


def passed_along(value, axis, steps):
    count = lax.axis_size(axis)
    pairs = [(source, (source + steps) % count) for source in range(count)]
    return lax.ppermute(value, axis, pairs)


def split(x):
    hi = x.astype(jnp.bfloat16)
    lo = (x - hi.astype(jnp.float32)).astype(jnp.bfloat16)
    return hi, lo


def stack_lhs(x):
    hi, lo = split(x)
    return jnp.concatenate([hi, hi, lo], axis=1)


def stack_rhs(y):
    hi, lo = split(y)
    return jnp.concatenate([hi, lo, hi], axis=0)


def triple_kernel(
    coupling_slots, interp_slots, blocks, region,
    idx_ref, a_ref, low_ref, mid_ref, up_ref, lo_ref, own_ref, hi_ref,
    y_ref, acc_ref, p3_ref,
):
    g = pl.program_id(0)
    steps = pl.num_programs(0)
    per_step = a_ref.shape[0]
    rows = steps * per_step
    bs = a_ref.shape[2]
    slot_base = rows * coupling_slots
    owner_base = slot_base + rows * coupling_slots * interp_slots

    @pl.when(g == 0)
    def _():
        acc_ref[...] = jnp.zeros_like(acc_ref)

        def fill(src, offset, count):
            def body(r, carry):
                for p in range(interp_slots):
                    hi, lo = split(src[r, p])
                    cols = slice(p * bs, (p + 1) * bs)
                    p3_ref[offset + r, 0:bs, cols] = hi
                    p3_ref[offset + r, bs : 2 * bs, cols] = lo
                    p3_ref[offset + r, 2 * bs : 3 * bs, cols] = hi
                return carry

            lax.fori_loop(0, count, body, 0)

        fill(low_ref, 0, RIM)
        fill(mid_ref, RIM, rows)
        fill(up_ref, RIM + rows, RIM)

    def row_step(i, carry):
        gi = g * per_step + i
        y_ref[...] = jnp.zeros_like(y_ref)
        for a in range(coupling_slots):
            row = idx_ref[gi * coupling_slots + a]
            prod = jnp.dot(stack_lhs(a_ref[i, a]), p3_ref[row], preferred_element_type=jnp.float32)
            for p in range(interp_slots):
                slot = idx_ref[slot_base + (gi * coupling_slots + a) * interp_slots + p]
                y_ref[slot] += prod[:, p * bs : (p + 1) * bs]
        pt = stack_lhs(jnp.concatenate([mid_ref[gi, q].T for q in range(interp_slots)], axis=0))
        owners = [idx_ref[owner_base + gi * interp_slots + q] for q in range(interp_slots)]
        for c in range(region):
            res = jnp.dot(pt, stack_rhs(y_ref[c]), preferred_element_type=jnp.float32)
            for q in range(interp_slots):
                acc_ref[owners[q], c] += res[q * bs : (q + 1) * bs]
        return carry

    lax.fori_loop(0, per_step, row_step, 0)

    @pl.when(g == steps - 1)
    def _():
        lo_ref[...] = acc_ref[:blocks]
        own_ref[...] = acc_ref[blocks : 2 * blocks]
        hi_ref[...] = acc_ref[2 * blocks :]


def shards(a_tiles, a_cols, p_tiles, p_cols, c_cols):
    rows, coupling_slots, bs, _ = a_tiles.shape
    interp_slots = p_tiles.shape[1]
    blocks, pattern_slots = c_cols.shape
    tiles = lax.axis_size("tile")
    slabs = lax.axis_size("slab")
    t = lax.axis_index("tile")
    s = lax.axis_index("slab")
    device = s * tiles + t
    region = 9 * blocks

    ext_rows = rows + 2 * RIM

    def halo(first):
        keys = p_cols[first : first + RIM].astype(jnp.float32).reshape(1, 1, 1, RIM * interp_slots)
        key_tile = jnp.pad(keys, ((0, 0), (0, interp_slots - 1), (0, bs - 1), (0, bs - RIM * interp_slots)))
        return jnp.concatenate([p_tiles[first : first + RIM], key_tile], axis=0)

    low = lax.ppermute(halo(rows - RIM), "slab", [(i, i + 1) for i in range(slabs - 1)])
    up = lax.ppermute(halo(0), "slab", [(i + 1, i) for i in range(slabs - 1)])

    def halo_keys(block):
        return block[RIM, 0, 0, : RIM * interp_slots].astype(jnp.int32).reshape(RIM, interp_slots)

    ext_keys = jnp.concatenate([halo_keys(low), p_cols, halo_keys(up)], axis=0)

    own_base = device * rows
    lower_base = (device - tiles) * rows + rows - RIM
    upper_base = (device + tiles) * rows
    local_index = jnp.where(
        a_cols < own_base,
        a_cols - lower_base,
        jnp.where(
            a_cols < own_base + rows,
            RIM + a_cols - own_base,
            RIM + rows + a_cols - upper_base,
        ),
    )
    local_index = jnp.clip(local_index, 0, ext_rows - 1)
    keys = ext_keys[local_index]
    k_slab = keys // (tiles * blocks)
    k_tile = (keys // blocks) % tiles
    k_dt = (k_tile - t + 1) % tiles - 1
    slot = ((k_slab - s + 1) * 3 + (k_dt + 1)) * blocks + keys % blocks
    slot = jnp.clip(slot, 0, region - 1)

    targets = p_cols - s * tiles * blocks
    relative = jnp.remainder(targets // blocks - t + 1, tiles)
    owner = jnp.clip(relative * blocks + targets % blocks, 0, 3 * blocks - 1)

    per_step = next(d for d in (4, 2, 1) if rows % d == 0)
    kernel = functools.partial(triple_kernel, coupling_slots, interp_slots, blocks, region)
    part = jax.ShapeDtypeStruct((blocks, region, bs, bs), jnp.float32)
    part_spec = pl.BlockSpec((blocks, region, bs, bs), lambda g, *_: (0, 0, 0, 0))
    table = jnp.concatenate(
        [local_index.reshape(-1), slot.reshape(-1), owner.reshape(-1)]
    ).astype(jnp.int32)
    to_lower, own_part, to_upper = pl.pallas_call(
        kernel,
        out_shape=(part, part, part),
        grid_spec=pltpu.PrefetchScalarGridSpec(
            num_scalar_prefetch=1,
            grid=(rows // per_step,),
            in_specs=[
                pl.BlockSpec((per_step, coupling_slots, bs, bs), lambda g, *_: (g, 0, 0, 0)),
                pl.BlockSpec(low.shape, lambda g, *_: (0, 0, 0, 0)),
                pl.BlockSpec(p_tiles.shape, lambda g, *_: (0, 0, 0, 0)),
                pl.BlockSpec(up.shape, lambda g, *_: (0, 0, 0, 0)),
            ],
            out_specs=(part_spec, part_spec, part_spec),
            scratch_shapes=[
                pltpu.VMEM((region, bs, bs), jnp.float32),
                pltpu.VMEM((3 * blocks, region, bs, bs), jnp.float32),
                pltpu.VMEM((ext_rows, 3 * bs, interp_slots * bs), jnp.bfloat16),
            ],
        ),
        compiler_params=pltpu.CompilerParams(dimension_semantics=("arbitrary",)),
    )(table, a_tiles, low, p_tiles, up)

    from_lower = passed_along(to_upper, "tile", 1)
    from_upper = passed_along(to_lower, "tile", -1)

    c_slab = c_cols // (tiles * blocks)
    c_tile = (c_cols // blocks) % tiles
    c_w = c_cols % blocks
    c_ds = (c_slab - s + 1) % slabs - 1
    c_dt = (c_tile - t + 2) % tiles - 2
    base = (c_ds + 1) * 3
    r_idx = jnp.arange(blocks, dtype=jnp.int32)[:, None]

    def pick(part, dt):
        valid = (dt >= -1) & (dt <= 1)
        idx = jnp.clip((base + dt + 1) * blocks + c_w, 0, region - 1)
        tiles_picked = part[r_idx, idx]
        return jnp.where(valid[:, :, None, None], tiles_picked, 0.0)

    early = lax.optimization_barrier(pick(own_part, c_dt) + pick(from_lower, c_dt + 1))
    return early + pick(from_upper, c_dt - 1)


def solution(mesh):
    return jax.shard_map(
        shards,
        mesh=mesh,
        in_specs=(
            P(("slab", "tile"), None, None, None),
            P(("slab", "tile"), None),
            P(("slab", "tile"), None, None, None),
            P(("slab", "tile"), None),
            P(("slab", "tile"), None),
        ),
        out_specs=P(("slab", "tile"), None, None, None),
        check_vma=False,
    )
```

```python
import functools

import jax
import jax.numpy as jnp
from jax import lax
from jax.experimental import pallas as pl
from jax.experimental.pallas import tpu as pltpu
from jax.sharding import PartitionSpec as P

RIM = 4


def passed_along(value, axis, steps):
    count = lax.axis_size(axis)
    pairs = [(source, (source + steps) % count) for source in range(count)]
    return lax.ppermute(value, axis, pairs)


def split(x):
    hi = x.astype(jnp.bfloat16)
    lo = (x - hi.astype(jnp.float32)).astype(jnp.bfloat16)
    return hi, lo


def stack_lhs(x):
    hi, lo = split(x)
    return jnp.concatenate([hi, hi, lo], axis=1)


def stack_rhs(y):
    hi, lo = split(y)
    return jnp.concatenate([hi, lo, hi], axis=0)


def triple_kernel(
    coupling_slots, interp_slots, blocks, region,
    idx_ref, a_ref, low_ref, mid_ref, up_ref, lo_ref, own_ref, hi_ref,
    y_ref, acc_ref, p3_ref,
):
    g = pl.program_id(0)
    steps = pl.num_programs(0)
    per_step = a_ref.shape[0]
    rows = steps * per_step
    bs = a_ref.shape[2]
    slot_base = rows * coupling_slots
    owner_base = slot_base + rows * coupling_slots * interp_slots

    @pl.when(g == 0)
    def _():
        acc_ref[...] = jnp.zeros_like(acc_ref)

        def fill(src, offset, count):
            def body(r, carry):
                for p in range(interp_slots):
                    hi, lo = split(src[r, p])
                    cols = slice(p * bs, (p + 1) * bs)
                    p3_ref[offset + r, 0:bs, cols] = hi
                    p3_ref[offset + r, bs : 2 * bs, cols] = lo
                    p3_ref[offset + r, 2 * bs : 3 * bs, cols] = hi
                return carry

            lax.fori_loop(0, count, body, 0)

        fill(low_ref, 0, RIM)
        fill(mid_ref, RIM, rows)
        fill(up_ref, RIM + rows, RIM)

    def row_step(i, carry):
        gi = g * per_step + i
        y_ref[...] = jnp.zeros_like(y_ref)
        for a in range(coupling_slots):
            row = idx_ref[gi * coupling_slots + a]
            prod = jnp.dot(stack_lhs(a_ref[i, a]), p3_ref[row], preferred_element_type=jnp.float32)
            for p in range(interp_slots):
                slot = idx_ref[slot_base + (gi * coupling_slots + a) * interp_slots + p]
                y_ref[slot] += prod[:, p * bs : (p + 1) * bs]
        pt = stack_lhs(jnp.concatenate([mid_ref[gi, q].T for q in range(interp_slots)], axis=0))
        owners = [idx_ref[owner_base + gi * interp_slots + q] for q in range(interp_slots)]
        for c in range(region):
            res = jnp.dot(pt, stack_rhs(y_ref[c]), preferred_element_type=jnp.float32)
            for q in range(interp_slots):
                acc_ref[owners[q], c] += res[q * bs : (q + 1) * bs]
        return carry

    lax.fori_loop(0, per_step, row_step, 0)

    @pl.when(g == steps - 1)
    def _():
        lo_ref[...] = acc_ref[:blocks]
        own_ref[...] = acc_ref[blocks : 2 * blocks]
        hi_ref[...] = acc_ref[2 * blocks :]


def shards(a_tiles, a_cols, p_tiles, p_cols, c_cols):
    rows, coupling_slots, bs, _ = a_tiles.shape
    interp_slots = p_tiles.shape[1]
    blocks, pattern_slots = c_cols.shape
    tiles = lax.axis_size("tile")
    slabs = lax.axis_size("slab")
    t = lax.axis_index("tile")
    s = lax.axis_index("slab")
    device = s * tiles + t
    region = 9 * blocks

    ext_rows = rows + 2 * RIM

    up_pairs = [(i, i + 1) for i in range(slabs - 1)]
    down_pairs = [(i + 1, i) for i in range(slabs - 1)]
    low = lax.ppermute(p_tiles[rows - RIM :], "slab", up_pairs)
    up = lax.ppermute(p_tiles[:RIM], "slab", down_pairs)
    low_keys = lax.ppermute(p_cols[rows - RIM :], "slab", up_pairs)
    up_keys = lax.ppermute(p_cols[:RIM], "slab", down_pairs)

    ext_keys = jnp.concatenate([low_keys, p_cols, up_keys], axis=0)

    own_base = device * rows
    lower_base = (device - tiles) * rows + rows - RIM
    upper_base = (device + tiles) * rows
    local_index = jnp.where(
        a_cols < own_base,
        a_cols - lower_base,
        jnp.where(
            a_cols < own_base + rows,
            RIM + a_cols - own_base,
            RIM + rows + a_cols - upper_base,
        ),
    )
    local_index = jnp.clip(local_index, 0, ext_rows - 1)
    keys = ext_keys[local_index]
    k_slab = keys // (tiles * blocks)
    k_tile = (keys // blocks) % tiles
    k_dt = (k_tile - t + 1) % tiles - 1
    slot = ((k_slab - s + 1) * 3 + (k_dt + 1)) * blocks + keys % blocks
    slot = jnp.clip(slot, 0, region - 1)

    targets = p_cols - s * tiles * blocks
    relative = jnp.remainder(targets // blocks - t + 1, tiles)
    owner = jnp.clip(relative * blocks + targets % blocks, 0, 3 * blocks - 1)

    per_step = next(d for d in (4, 2, 1) if rows % d == 0)
    kernel = functools.partial(triple_kernel, coupling_slots, interp_slots, blocks, region)
    part = jax.ShapeDtypeStruct((blocks, region, bs, bs), jnp.float32)
    part_spec = pl.BlockSpec((blocks, region, bs, bs), lambda g, *_: (0, 0, 0, 0))
    table = jnp.concatenate(
        [local_index.reshape(-1), slot.reshape(-1), owner.reshape(-1)]
    ).astype(jnp.int32)
    to_lower, own_part, to_upper = pl.pallas_call(
        kernel,
        out_shape=(part, part, part),
        grid_spec=pltpu.PrefetchScalarGridSpec(
            num_scalar_prefetch=1,
            grid=(rows // per_step,),
            in_specs=[
                pl.BlockSpec((per_step, coupling_slots, bs, bs), lambda g, *_: (g, 0, 0, 0)),
                pl.BlockSpec(low.shape, lambda g, *_: (0, 0, 0, 0)),
                pl.BlockSpec(p_tiles.shape, lambda g, *_: (0, 0, 0, 0)),
                pl.BlockSpec(up.shape, lambda g, *_: (0, 0, 0, 0)),
            ],
            out_specs=(part_spec, part_spec, part_spec),
            scratch_shapes=[
                pltpu.VMEM((region, bs, bs), jnp.float32),
                pltpu.VMEM((3 * blocks, region, bs, bs), jnp.float32),
                pltpu.VMEM((ext_rows, 3 * bs, interp_slots * bs), jnp.bfloat16),
            ],
        ),
        compiler_params=pltpu.CompilerParams(dimension_semantics=("arbitrary",)),
    )(table, a_tiles, low, p_tiles, up)

    from_lower = passed_along(to_upper, "tile", 1)
    from_upper = passed_along(to_lower, "tile", -1)

    c_slab = c_cols // (tiles * blocks)
    c_tile = (c_cols // blocks) % tiles
    c_w = c_cols % blocks
    c_ds = (c_slab - s + 1) % slabs - 1
    c_dt = (c_tile - t + 2) % tiles - 2
    base = (c_ds + 1) * 3
    r_idx = jnp.arange(blocks, dtype=jnp.int32)[:, None]

    def pick(part, dt):
        valid = (dt >= -1) & (dt <= 1)
        idx = jnp.clip((base + dt + 1) * blocks + c_w, 0, region - 1)
        tiles_picked = part[r_idx, idx]
        return jnp.where(valid[:, :, None, None], tiles_picked, 0.0)

    early = lax.optimization_barrier(pick(own_part, c_dt) + pick(from_lower, c_dt + 1))
    return early + pick(from_upper, c_dt - 1)


def solution(mesh):
    return jax.shard_map(
        shards,
        mesh=mesh,
        in_specs=(
            P(("slab", "tile"), None, None, None),
            P(("slab", "tile"), None),
            P(("slab", "tile"), None, None, None),
            P(("slab", "tile"), None),
            P(("slab", "tile"), None),
        ),
        out_specs=P(("slab", "tile"), None, None, None),
        check_vma=False,
    )
```

```python
import functools

import jax
import jax.numpy as jnp
from jax import lax
from jax.experimental import pallas as pl
from jax.experimental.pallas import tpu as pltpu
from jax.sharding import PartitionSpec as P

RIM = 4
HIGH = lax.Precision.HIGH


def passed_along(value, axis, steps):
    count = lax.axis_size(axis)
    pairs = [(source, (source + steps) % count) for source in range(count)]
    return lax.ppermute(value, axis, pairs)


def split(x):
    hi = x.astype(jnp.bfloat16)
    lo = (x - hi.astype(jnp.float32)).astype(jnp.bfloat16)
    return hi, lo


def stack_lhs(x):
    hi, lo = split(x)
    return jnp.concatenate([hi, hi, lo], axis=1)


def stack_rhs(y):
    hi, lo = split(y)
    return jnp.concatenate([hi, lo, hi], axis=0)


def triple_kernel(
    coupling_slots, interp_slots, blocks, region,
    idx_ref, a_ref, low_ref, mid_ref, up_ref, lo_ref, own_ref, hi_ref,
    y_ref, acc_ref, p3_ref,
):
    g = pl.program_id(0)
    steps = pl.num_programs(0)
    per_step = a_ref.shape[0]
    rows = steps * per_step
    bs = a_ref.shape[2]
    slot_base = rows * coupling_slots
    owner_base = slot_base + rows * coupling_slots * interp_slots

    @pl.when(g == 0)
    def _():
        acc_ref[...] = jnp.zeros_like(acc_ref)

        def fill(src, offset, count):
            def body(r, carry):
                for p in range(interp_slots):
                    p3_ref[offset + r, :, p * bs : (p + 1) * bs] = src[r, p]
                return carry

            lax.fori_loop(0, count, body, 0)

        fill(low_ref, 0, RIM)
        fill(mid_ref, RIM, rows)
        fill(up_ref, RIM + rows, RIM)

    def row_step(i, carry):
        gi = g * per_step + i
        y_ref[...] = jnp.zeros_like(y_ref)
        for a in range(coupling_slots):
            row = idx_ref[gi * coupling_slots + a]
            prod = jnp.dot(a_ref[i, a], p3_ref[row], precision=HIGH, preferred_element_type=jnp.float32)
            for p in range(interp_slots):
                slot = idx_ref[slot_base + (gi * coupling_slots + a) * interp_slots + p]
                y_ref[slot] += prod[:, p * bs : (p + 1) * bs]
        pt = jnp.concatenate([mid_ref[gi, q].T for q in range(interp_slots)], axis=0)
        owners = [idx_ref[owner_base + gi * interp_slots + q] for q in range(interp_slots)]
        for c in range(region):
            res = jnp.dot(pt, y_ref[c], precision=HIGH, preferred_element_type=jnp.float32)
            for q in range(interp_slots):
                acc_ref[owners[q], c] += res[q * bs : (q + 1) * bs]
        return carry

    lax.fori_loop(0, per_step, row_step, 0)

    @pl.when(g == steps - 1)
    def _():
        lo_ref[...] = acc_ref[:blocks]
        own_ref[...] = acc_ref[blocks : 2 * blocks]
        hi_ref[...] = acc_ref[2 * blocks :]


def shards(a_tiles, a_cols, p_tiles, p_cols, c_cols):
    rows, coupling_slots, bs, _ = a_tiles.shape
    interp_slots = p_tiles.shape[1]
    blocks, pattern_slots = c_cols.shape
    tiles = lax.axis_size("tile")
    slabs = lax.axis_size("slab")
    t = lax.axis_index("tile")
    s = lax.axis_index("slab")
    device = s * tiles + t
    region = 9 * blocks

    ext_rows = rows + 2 * RIM

    def halo(first):
        keys = p_cols[first : first + RIM].astype(jnp.float32).reshape(1, 1, 1, RIM * interp_slots)
        key_tile = jnp.pad(keys, ((0, 0), (0, interp_slots - 1), (0, bs - 1), (0, bs - RIM * interp_slots)))
        return jnp.concatenate([p_tiles[first : first + RIM], key_tile], axis=0)

    low = lax.ppermute(halo(rows - RIM), "slab", [(i, i + 1) for i in range(slabs - 1)])
    up = lax.ppermute(halo(0), "slab", [(i + 1, i) for i in range(slabs - 1)])

    def halo_keys(block):
        return block[RIM, 0, 0, : RIM * interp_slots].astype(jnp.int32).reshape(RIM, interp_slots)

    ext_keys = jnp.concatenate([halo_keys(low), p_cols, halo_keys(up)], axis=0)

    own_base = device * rows
    lower_base = (device - tiles) * rows + rows - RIM
    upper_base = (device + tiles) * rows
    local_index = jnp.where(
        a_cols < own_base,
        a_cols - lower_base,
        jnp.where(
            a_cols < own_base + rows,
            RIM + a_cols - own_base,
            RIM + rows + a_cols - upper_base,
        ),
    )
    local_index = jnp.clip(local_index, 0, ext_rows - 1)
    keys = ext_keys[local_index]
    k_slab = keys // (tiles * blocks)
    k_tile = (keys // blocks) % tiles
    k_dt = (k_tile - t + 1) % tiles - 1
    slot = ((k_slab - s + 1) * 3 + (k_dt + 1)) * blocks + keys % blocks
    slot = jnp.clip(slot, 0, region - 1)

    targets = p_cols - s * tiles * blocks
    relative = jnp.remainder(targets // blocks - t + 1, tiles)
    owner = jnp.clip(relative * blocks + targets % blocks, 0, 3 * blocks - 1)

    per_step = next(d for d in (4, 2, 1) if rows % d == 0)
    kernel = functools.partial(triple_kernel, coupling_slots, interp_slots, blocks, region)
    part = jax.ShapeDtypeStruct((blocks, region, bs, bs), jnp.float32)
    part_spec = pl.BlockSpec((blocks, region, bs, bs), lambda g, *_: (0, 0, 0, 0))
    table = jnp.concatenate(
        [local_index.reshape(-1), slot.reshape(-1), owner.reshape(-1)]
    ).astype(jnp.int32)
    to_lower, own_part, to_upper = pl.pallas_call(
        kernel,
        out_shape=(part, part, part),
        grid_spec=pltpu.PrefetchScalarGridSpec(
            num_scalar_prefetch=1,
            grid=(rows // per_step,),
            in_specs=[
                pl.BlockSpec((per_step, coupling_slots, bs, bs), lambda g, *_: (g, 0, 0, 0)),
                pl.BlockSpec(low.shape, lambda g, *_: (0, 0, 0, 0)),
                pl.BlockSpec(p_tiles.shape, lambda g, *_: (0, 0, 0, 0)),
                pl.BlockSpec(up.shape, lambda g, *_: (0, 0, 0, 0)),
            ],
            out_specs=(part_spec, part_spec, part_spec),
            scratch_shapes=[
                pltpu.VMEM((region, bs, bs), jnp.float32),
                pltpu.VMEM((3 * blocks, region, bs, bs), jnp.float32),
                pltpu.VMEM((ext_rows, bs, interp_slots * bs), jnp.float32),
            ],
        ),
        compiler_params=pltpu.CompilerParams(dimension_semantics=("arbitrary",)),
    )(table, a_tiles, low, p_tiles, up)

    from_lower = passed_along(to_upper, "tile", 1)
    from_upper = passed_along(to_lower, "tile", -1)

    c_slab = c_cols // (tiles * blocks)
    c_tile = (c_cols // blocks) % tiles
    c_w = c_cols % blocks
    c_ds = (c_slab - s + 1) % slabs - 1
    c_dt = (c_tile - t + 2) % tiles - 2
    base = (c_ds + 1) * 3
    r_idx = jnp.arange(blocks, dtype=jnp.int32)[:, None]

    def pick(part, dt):
        valid = (dt >= -1) & (dt <= 1)
        idx = jnp.clip((base + dt + 1) * blocks + c_w, 0, region - 1)
        tiles_picked = part[r_idx, idx]
        return jnp.where(valid[:, :, None, None], tiles_picked, 0.0)

    early = lax.optimization_barrier(pick(own_part, c_dt) + pick(from_lower, c_dt + 1))
    return early + pick(from_upper, c_dt - 1)


def solution(mesh):
    return jax.shard_map(
        shards,
        mesh=mesh,
        in_specs=(
            P(("slab", "tile"), None, None, None),
            P(("slab", "tile"), None),
            P(("slab", "tile"), None, None, None),
            P(("slab", "tile"), None),
            P(("slab", "tile"), None),
        ),
        out_specs=P(("slab", "tile"), None, None, None),
        check_vma=False,
    )
```

```python
import functools

import jax
import jax.numpy as jnp
from jax import lax
from jax.experimental import pallas as pl
from jax.experimental.pallas import tpu as pltpu
from jax.sharding import PartitionSpec as P

RIM = 4


def passed_along(value, axis, steps):
    count = lax.axis_size(axis)
    pairs = [(source, (source + steps) % count) for source in range(count)]
    return lax.ppermute(value, axis, pairs)


def split(x):
    hi = x.astype(jnp.bfloat16)
    lo = (x - hi.astype(jnp.float32)).astype(jnp.bfloat16)
    return hi, lo


def stack_lhs(x):
    hi, lo = split(x)
    return jnp.concatenate([hi, hi, lo], axis=1)


def stack_rhs(y):
    hi, lo = split(y)
    return jnp.concatenate([hi, lo, hi], axis=0)


def triple_kernel(
    coupling_slots, interp_slots, blocks, region,
    idx_ref, a_ref, low_ref, mid_ref, up_ref, lo_ref, own_ref, hi_ref,
    y_ref, acc_ref, p3_ref,
):
    g = pl.program_id(0)
    steps = pl.num_programs(0)
    per_step = a_ref.shape[0]
    rows = steps * per_step
    bs = a_ref.shape[2]
    slot_base = rows * coupling_slots
    owner_base = slot_base + rows * coupling_slots * interp_slots

    @pl.when(g == 0)
    def _():
        acc_ref[...] = jnp.zeros_like(acc_ref)

        def fill(src, offset, count):
            def body(r, carry):
                for p in range(interp_slots):
                    if len(src.shape) == 2:
                        start = pl.multiple_of((r * interp_slots + p) * bs, bs)
                        tile = src[pl.ds(start, bs), :]
                    else:
                        tile = src[r, p]
                    hi, lo = split(tile)
                    cols = slice(p * bs, (p + 1) * bs)
                    p3_ref[offset + r, 0:bs, cols] = hi
                    p3_ref[offset + r, bs : 2 * bs, cols] = lo
                    p3_ref[offset + r, 2 * bs : 3 * bs, cols] = hi
                return carry

            lax.fori_loop(0, count, body, 0)

        fill(low_ref, 0, RIM)
        fill(mid_ref, RIM, rows)
        fill(up_ref, RIM + rows, RIM)

    def row_step(i, carry):
        gi = g * per_step + i
        y_ref[...] = jnp.zeros_like(y_ref)
        for a in range(coupling_slots):
            row = idx_ref[gi * coupling_slots + a]
            prod = jnp.dot(stack_lhs(a_ref[i, a]), p3_ref[row], preferred_element_type=jnp.float32)
            for p in range(interp_slots):
                slot = idx_ref[slot_base + (gi * coupling_slots + a) * interp_slots + p]
                y_ref[slot] += prod[:, p * bs : (p + 1) * bs]
        pt = stack_lhs(jnp.concatenate([mid_ref[gi, q].T for q in range(interp_slots)], axis=0))
        owners = [idx_ref[owner_base + gi * interp_slots + q] for q in range(interp_slots)]
        for c in range(region):
            res = jnp.dot(pt, stack_rhs(y_ref[c]), preferred_element_type=jnp.float32)
            for q in range(interp_slots):
                acc_ref[owners[q], c] += res[q * bs : (q + 1) * bs]
        return carry

    lax.fori_loop(0, per_step, row_step, 0)

    @pl.when(g == steps - 1)
    def _():
        lo_ref[...] = acc_ref[:blocks]
        own_ref[...] = acc_ref[blocks : 2 * blocks]
        hi_ref[...] = acc_ref[2 * blocks :]


def shards(a_tiles, a_cols, p_tiles, p_cols, c_cols):
    rows, coupling_slots, bs, _ = a_tiles.shape
    interp_slots = p_tiles.shape[1]
    blocks, pattern_slots = c_cols.shape
    tiles = lax.axis_size("tile")
    slabs = lax.axis_size("slab")
    t = lax.axis_index("tile")
    s = lax.axis_index("slab")
    device = s * tiles + t
    region = 9 * blocks

    ext_rows = rows + 2 * RIM

    key_count = RIM * interp_slots

    def halo(first):
        keys = p_cols[first : first + RIM].astype(jnp.float32).reshape(1, key_count)
        key_rows = jnp.pad(keys, ((0, 7), (0, bs - key_count)))
        flat = p_tiles[first : first + RIM].reshape(RIM * interp_slots * bs, bs)
        return jnp.concatenate([flat, key_rows], axis=0)

    low = lax.ppermute(halo(rows - RIM), "slab", [(i, i + 1) for i in range(slabs - 1)])
    up = lax.ppermute(halo(0), "slab", [(i + 1, i) for i in range(slabs - 1)])

    def halo_keys(block):
        return block[key_count * bs, :key_count].astype(jnp.int32).reshape(RIM, interp_slots)

    ext_keys = jnp.concatenate([halo_keys(low), p_cols, halo_keys(up)], axis=0)

    own_base = device * rows
    lower_base = (device - tiles) * rows + rows - RIM
    upper_base = (device + tiles) * rows
    local_index = jnp.where(
        a_cols < own_base,
        a_cols - lower_base,
        jnp.where(
            a_cols < own_base + rows,
            RIM + a_cols - own_base,
            RIM + rows + a_cols - upper_base,
        ),
    )
    local_index = jnp.clip(local_index, 0, ext_rows - 1)
    keys = ext_keys[local_index]
    k_slab = keys // (tiles * blocks)
    k_tile = (keys // blocks) % tiles
    k_dt = (k_tile - t + 1) % tiles - 1
    slot = ((k_slab - s + 1) * 3 + (k_dt + 1)) * blocks + keys % blocks
    slot = jnp.clip(slot, 0, region - 1)

    targets = p_cols - s * tiles * blocks
    relative = jnp.remainder(targets // blocks - t + 1, tiles)
    owner = jnp.clip(relative * blocks + targets % blocks, 0, 3 * blocks - 1)

    per_step = next(d for d in (4, 2, 1) if rows % d == 0)
    kernel = functools.partial(triple_kernel, coupling_slots, interp_slots, blocks, region)
    part = jax.ShapeDtypeStruct((blocks, region, bs, bs), jnp.float32)
    part_spec = pl.BlockSpec((blocks, region, bs, bs), lambda g, *_: (0, 0, 0, 0))
    table = jnp.concatenate(
        [local_index.reshape(-1), slot.reshape(-1), owner.reshape(-1)]
    ).astype(jnp.int32)
    to_lower, own_part, to_upper = pl.pallas_call(
        kernel,
        out_shape=(part, part, part),
        grid_spec=pltpu.PrefetchScalarGridSpec(
            num_scalar_prefetch=1,
            grid=(rows // per_step,),
            in_specs=[
                pl.BlockSpec((per_step, coupling_slots, bs, bs), lambda g, *_: (g, 0, 0, 0)),
                pl.BlockSpec(low.shape, lambda g, *_: (0, 0)),
                pl.BlockSpec(p_tiles.shape, lambda g, *_: (0, 0, 0, 0)),
                pl.BlockSpec(up.shape, lambda g, *_: (0, 0)),
            ],
            out_specs=(part_spec, part_spec, part_spec),
            scratch_shapes=[
                pltpu.VMEM((region, bs, bs), jnp.float32),
                pltpu.VMEM((3 * blocks, region, bs, bs), jnp.float32),
                pltpu.VMEM((ext_rows, 3 * bs, interp_slots * bs), jnp.bfloat16),
            ],
        ),
        compiler_params=pltpu.CompilerParams(dimension_semantics=("arbitrary",)),
    )(table, a_tiles, low, p_tiles, up)

    from_lower = passed_along(to_upper, "tile", 1)
    from_upper = passed_along(to_lower, "tile", -1)

    c_slab = c_cols // (tiles * blocks)
    c_tile = (c_cols // blocks) % tiles
    c_w = c_cols % blocks
    c_ds = (c_slab - s + 1) % slabs - 1
    c_dt = (c_tile - t + 2) % tiles - 2
    base = (c_ds + 1) * 3
    r_idx = jnp.arange(blocks, dtype=jnp.int32)[:, None]

    def pick(part, dt):
        valid = (dt >= -1) & (dt <= 1)
        idx = jnp.clip((base + dt + 1) * blocks + c_w, 0, region - 1)
        tiles_picked = part[r_idx, idx]
        return jnp.where(valid[:, :, None, None], tiles_picked, 0.0)

    early = lax.optimization_barrier(pick(own_part, c_dt) + pick(from_lower, c_dt + 1))
    return early + pick(from_upper, c_dt - 1)


def solution(mesh):
    return jax.shard_map(
        shards,
        mesh=mesh,
        in_specs=(
            P(("slab", "tile"), None, None, None),
            P(("slab", "tile"), None),
            P(("slab", "tile"), None, None, None),
            P(("slab", "tile"), None),
            P(("slab", "tile"), None),
        ),
        out_specs=P(("slab", "tile"), None, None, None),
        check_vma=False,
    )
```

```python
import functools

import jax
import jax.numpy as jnp
from jax import lax
from jax.experimental import pallas as pl
from jax.experimental.pallas import tpu as pltpu
from jax.sharding import PartitionSpec as P

RIM = 4


def passed_along(value, axis, steps):
    count = lax.axis_size(axis)
    pairs = [(source, (source + steps) % count) for source in range(count)]
    return lax.ppermute(value, axis, pairs)


def split(x):
    hi = x.astype(jnp.bfloat16)
    lo = (x - hi.astype(jnp.float32)).astype(jnp.bfloat16)
    return hi, lo


def stack_lhs(x):
    hi, lo = split(x)
    return jnp.concatenate([hi, hi, lo], axis=1)


def stack_rhs(y):
    hi, lo = split(y)
    return jnp.concatenate([hi, lo, hi], axis=0)


def triple_kernel(
    coupling_slots, interp_slots, blocks, region,
    idx_ref, a_ref, low_ref, mid_ref, up_ref, lo_ref, own_ref, hi_ref,
    y_ref, acc_ref, p3_ref,
):
    g = pl.program_id(0)
    steps = pl.num_programs(0)
    per_step = a_ref.shape[0]
    rows = steps * per_step
    bs = a_ref.shape[2]
    slot_base = rows * coupling_slots
    owner_base = slot_base + rows * coupling_slots * interp_slots

    @pl.when(g == 0)
    def _():
        acc_ref[...] = jnp.zeros_like(acc_ref)

        def fill(src, offset, count):
            def body(r, carry):
                for p in range(interp_slots):
                    if len(src.shape) == 2:
                        start = pl.multiple_of((r * interp_slots + p) * bs, bs)
                        tile = src[pl.ds(start, bs), :]
                    else:
                        tile = src[r, p]
                    hi, lo = split(tile)
                    cols = slice(p * bs, (p + 1) * bs)
                    p3_ref[offset + r, 0:bs, cols] = hi
                    p3_ref[offset + r, bs : 2 * bs, cols] = lo
                    p3_ref[offset + r, 2 * bs : 3 * bs, cols] = hi
                return carry

            lax.fori_loop(0, count, body, 0)

        fill(low_ref, 0, RIM)
        fill(mid_ref, RIM, rows)
        fill(up_ref, RIM + rows, RIM)

    def row_step(i, carry):
        gi = g * per_step + i
        y_ref[...] = jnp.zeros_like(y_ref)
        for a in range(coupling_slots):
            row = idx_ref[gi * coupling_slots + a]
            prod = jnp.dot(stack_lhs(a_ref[i, a]), p3_ref[row], preferred_element_type=jnp.float32)
            for p in range(interp_slots):
                slot = idx_ref[slot_base + (gi * coupling_slots + a) * interp_slots + p]
                y_ref[slot] += prod[:, p * bs : (p + 1) * bs]
        pt = stack_lhs(jnp.concatenate([mid_ref[gi, q].T for q in range(interp_slots)], axis=0))
        owners = [idx_ref[owner_base + gi * interp_slots + q] for q in range(interp_slots)]
        for c in range(region):
            res = jnp.dot(pt, stack_rhs(y_ref[c]), preferred_element_type=jnp.float32)
            for q in range(interp_slots):
                acc_ref[owners[q], c] += res[q * bs : (q + 1) * bs]
        return carry

    lax.fori_loop(0, per_step, row_step, 0)

    @pl.when(g == steps - 1)
    def _():
        lo_ref[...] = acc_ref[:blocks]
        own_ref[...] = acc_ref[blocks : 2 * blocks]
        hi_ref[...] = acc_ref[2 * blocks :]


def shards(a_tiles, a_cols, p_tiles, p_cols, c_cols):
    rows, coupling_slots, bs, _ = a_tiles.shape
    interp_slots = p_tiles.shape[1]
    blocks, pattern_slots = c_cols.shape
    tiles = lax.axis_size("tile")
    slabs = lax.axis_size("slab")
    t = lax.axis_index("tile")
    s = lax.axis_index("slab")
    device = s * tiles + t
    region = 9 * blocks

    ext_rows = rows + 2 * RIM

    key_count = RIM * interp_slots

    def halo(first):
        keys = p_cols[first : first + RIM].astype(jnp.float32).reshape(1, key_count)
        key_rows = jnp.pad(keys, ((0, 7), (0, bs - key_count)))
        flat = p_tiles[first : first + RIM].reshape(RIM * interp_slots * bs, bs)
        return jnp.concatenate([flat, key_rows], axis=0)

    low = lax.ppermute(halo(rows - RIM), "slab", [(i, i + 1) for i in range(slabs - 1)])
    up = lax.ppermute(halo(0), "slab", [(i + 1, i) for i in range(slabs - 1)])

    def halo_keys(block):
        return block[key_count * bs, :key_count].astype(jnp.int32).reshape(RIM, interp_slots)

    ext_keys = jnp.concatenate([halo_keys(low), p_cols, halo_keys(up)], axis=0)

    own_base = device * rows
    lower_base = (device - tiles) * rows + rows - RIM
    upper_base = (device + tiles) * rows
    local_index = jnp.where(
        a_cols < own_base,
        a_cols - lower_base,
        jnp.where(
            a_cols < own_base + rows,
            RIM + a_cols - own_base,
            RIM + rows + a_cols - upper_base,
        ),
    )
    local_index = jnp.clip(local_index, 0, ext_rows - 1)
    keys = ext_keys[local_index]
    k_slab = keys // (tiles * blocks)
    k_tile = (keys // blocks) % tiles
    k_dt = (k_tile - t + 1) % tiles - 1
    slot = ((k_slab - s + 1) * 3 + (k_dt + 1)) * blocks + keys % blocks
    slot = jnp.clip(slot, 0, region - 1)

    targets = p_cols - s * tiles * blocks
    relative = jnp.remainder(targets // blocks - t + 1, tiles)
    owner = jnp.clip(relative * blocks + targets % blocks, 0, 3 * blocks - 1)

    per_step = next(d for d in (2, 1) if rows % d == 0)
    kernel = functools.partial(triple_kernel, coupling_slots, interp_slots, blocks, region)
    part = jax.ShapeDtypeStruct((blocks, region, bs, bs), jnp.float32)
    part_spec = pl.BlockSpec((blocks, region, bs, bs), lambda g, *_: (0, 0, 0, 0))
    table = jnp.concatenate(
        [local_index.reshape(-1), slot.reshape(-1), owner.reshape(-1)]
    ).astype(jnp.int32)
    to_lower, own_part, to_upper = pl.pallas_call(
        kernel,
        out_shape=(part, part, part),
        grid_spec=pltpu.PrefetchScalarGridSpec(
            num_scalar_prefetch=1,
            grid=(rows // per_step,),
            in_specs=[
                pl.BlockSpec((per_step, coupling_slots, bs, bs), lambda g, *_: (g, 0, 0, 0)),
                pl.BlockSpec(low.shape, lambda g, *_: (0, 0)),
                pl.BlockSpec(p_tiles.shape, lambda g, *_: (0, 0, 0, 0)),
                pl.BlockSpec(up.shape, lambda g, *_: (0, 0)),
            ],
            out_specs=(part_spec, part_spec, part_spec),
            scratch_shapes=[
                pltpu.VMEM((region, bs, bs), jnp.float32),
                pltpu.VMEM((3 * blocks, region, bs, bs), jnp.float32),
                pltpu.VMEM((ext_rows, 3 * bs, interp_slots * bs), jnp.bfloat16),
            ],
        ),
        compiler_params=pltpu.CompilerParams(dimension_semantics=("arbitrary",)),
    )(table, a_tiles, low, p_tiles, up)

    from_lower = passed_along(to_upper, "tile", 1)
    from_upper = passed_along(to_lower, "tile", -1)

    c_slab = c_cols // (tiles * blocks)
    c_tile = (c_cols // blocks) % tiles
    c_w = c_cols % blocks
    c_ds = (c_slab - s + 1) % slabs - 1
    c_dt = (c_tile - t + 2) % tiles - 2
    base = (c_ds + 1) * 3
    r_idx = jnp.arange(blocks, dtype=jnp.int32)[:, None]

    def pick(part, dt):
        valid = (dt >= -1) & (dt <= 1)
        idx = jnp.clip((base + dt + 1) * blocks + c_w, 0, region - 1)
        tiles_picked = part[r_idx, idx]
        return jnp.where(valid[:, :, None, None], tiles_picked, 0.0)

    early = lax.optimization_barrier(pick(own_part, c_dt) + pick(from_lower, c_dt + 1))
    return early + pick(from_upper, c_dt - 1)


def solution(mesh):
    return jax.shard_map(
        shards,
        mesh=mesh,
        in_specs=(
            P(("slab", "tile"), None, None, None),
            P(("slab", "tile"), None),
            P(("slab", "tile"), None, None, None),
            P(("slab", "tile"), None),
            P(("slab", "tile"), None),
        ),
        out_specs=P(("slab", "tile"), None, None, None),
        check_vma=False,
    )
```

```python
import functools

import jax
import jax.numpy as jnp
from jax import lax
from jax.experimental import pallas as pl
from jax.experimental.pallas import tpu as pltpu
from jax.sharding import PartitionSpec as P

RIM = 4


def passed_along(value, axis, steps):
    count = lax.axis_size(axis)
    pairs = [(source, (source + steps) % count) for source in range(count)]
    return lax.ppermute(value, axis, pairs)


def split(x):
    hi = x.astype(jnp.bfloat16)
    lo = (x - hi.astype(jnp.float32)).astype(jnp.bfloat16)
    return hi, lo


def stack_lhs(x):
    hi, lo = split(x)
    return jnp.concatenate([hi, hi, lo], axis=1)


def stack_rhs(y):
    hi, lo = split(y)
    return jnp.concatenate([hi, lo, hi], axis=0)


def triple_kernel(
    coupling_slots, interp_slots, blocks, region,
    idx_ref, rowslot_ref, a_ref, low_ref, mid_ref, up_ref, lo_ref, own_ref, hi_ref,
    y_ref, acc_ref, p3_ref,
):
    g = pl.program_id(0)
    steps = pl.num_programs(0)
    per_step = a_ref.shape[0]
    rows = steps * per_step
    bs = a_ref.shape[2]
    slot_base = rows * coupling_slots
    owner_base = slot_base

    @pl.when(g == 0)
    def _():
        acc_ref[...] = jnp.zeros_like(acc_ref)

        def fill(src, offset, count):
            def body(r, carry):
                for p in range(interp_slots):
                    if len(src.shape) == 2:
                        start = pl.multiple_of((r * interp_slots + p) * bs, bs)
                        tile = src[pl.ds(start, bs), :]
                    else:
                        tile = src[r, p]
                    hi, lo = split(tile)
                    cols = slice(p * bs, (p + 1) * bs)
                    p3_ref[offset + r, 0:bs, cols] = hi
                    p3_ref[offset + r, bs : 2 * bs, cols] = lo
                    p3_ref[offset + r, 2 * bs : 3 * bs, cols] = hi
                return carry

            lax.fori_loop(0, count, body, 0)

        fill(low_ref, 0, RIM)
        fill(mid_ref, RIM, rows)
        fill(up_ref, RIM + rows, RIM)

    def row_step(i, carry):
        gi = g * per_step + i
        y_ref[...] = jnp.zeros_like(y_ref)
        for a in range(coupling_slots):
            row = idx_ref[gi * coupling_slots + a]
            prod = jnp.dot(stack_lhs(a_ref[i, a]), p3_ref[row], preferred_element_type=jnp.float32)
            for p in range(interp_slots):
                slot = rowslot_ref[row * interp_slots + p]
                y_ref[slot] += prod[:, p * bs : (p + 1) * bs]
        pt = stack_lhs(jnp.concatenate([mid_ref[gi, q].T for q in range(interp_slots)], axis=0))
        owners = [idx_ref[owner_base + gi * interp_slots + q] for q in range(interp_slots)]
        for c in range(region):
            res = jnp.dot(pt, stack_rhs(y_ref[c]), preferred_element_type=jnp.float32)
            for q in range(interp_slots):
                acc_ref[owners[q], c] += res[q * bs : (q + 1) * bs]
        return carry

    lax.fori_loop(0, per_step, row_step, 0)

    @pl.when(g == steps - 1)
    def _():
        lo_ref[...] = acc_ref[:blocks]
        own_ref[...] = acc_ref[blocks : 2 * blocks]
        hi_ref[...] = acc_ref[2 * blocks :]


def shards(a_tiles, a_cols, p_tiles, p_cols, c_cols):
    rows, coupling_slots, bs, _ = a_tiles.shape
    interp_slots = p_tiles.shape[1]
    blocks, pattern_slots = c_cols.shape
    tiles = lax.axis_size("tile")
    slabs = lax.axis_size("slab")
    t = lax.axis_index("tile")
    s = lax.axis_index("slab")
    device = s * tiles + t
    region = 9 * blocks

    ext_rows = rows + 2 * RIM

    key_count = RIM * interp_slots

    def halo(first):
        keys = p_cols[first : first + RIM].astype(jnp.float32).reshape(1, key_count)
        key_rows = jnp.pad(keys, ((0, 7), (0, bs - key_count)))
        flat = p_tiles[first : first + RIM].reshape(RIM * interp_slots * bs, bs)
        return jnp.concatenate([flat, key_rows], axis=0)

    low = lax.ppermute(halo(rows - RIM), "slab", [(i, i + 1) for i in range(slabs - 1)])
    up = lax.ppermute(halo(0), "slab", [(i + 1, i) for i in range(slabs - 1)])

    def halo_keys(block):
        return block[key_count * bs, :key_count].astype(jnp.int32)

    ext_keys = jnp.concatenate([halo_keys(low), p_cols.reshape(-1), halo_keys(up)])

    own_base = device * rows
    lower_base = (device - tiles) * rows + rows - RIM
    upper_base = (device + tiles) * rows
    local_index = jnp.where(
        a_cols < own_base,
        a_cols - lower_base,
        jnp.where(
            a_cols < own_base + rows,
            RIM + a_cols - own_base,
            RIM + rows + a_cols - upper_base,
        ),
    )
    local_index = jnp.clip(local_index, 0, ext_rows - 1)
    keys = ext_keys
    k_slab = keys // (tiles * blocks)
    k_tile = (keys // blocks) % tiles
    k_dt = (k_tile - t + 1) % tiles - 1
    slot = ((k_slab - s + 1) * 3 + (k_dt + 1)) * blocks + keys % blocks
    slot = jnp.clip(slot, 0, region - 1).astype(jnp.int32)

    targets = p_cols - s * tiles * blocks
    relative = jnp.remainder(targets // blocks - t + 1, tiles)
    owner = jnp.clip(relative * blocks + targets % blocks, 0, 3 * blocks - 1)

    per_step = next(d for d in (2, 1) if rows % d == 0)
    kernel = functools.partial(triple_kernel, coupling_slots, interp_slots, blocks, region)
    part = jax.ShapeDtypeStruct((blocks, region, bs, bs), jnp.float32)
    part_spec = pl.BlockSpec((blocks, region, bs, bs), lambda g, *_: (0, 0, 0, 0))
    table = jnp.concatenate(
        [local_index.reshape(-1), owner.reshape(-1)]
    ).astype(jnp.int32)
    to_lower, own_part, to_upper = pl.pallas_call(
        kernel,
        out_shape=(part, part, part),
        grid_spec=pltpu.PrefetchScalarGridSpec(
            num_scalar_prefetch=2,
            grid=(rows // per_step,),
            in_specs=[
                pl.BlockSpec((per_step, coupling_slots, bs, bs), lambda g, *_: (g, 0, 0, 0)),
                pl.BlockSpec(low.shape, lambda g, *_: (0, 0)),
                pl.BlockSpec(p_tiles.shape, lambda g, *_: (0, 0, 0, 0)),
                pl.BlockSpec(up.shape, lambda g, *_: (0, 0)),
            ],
            out_specs=(part_spec, part_spec, part_spec),
            scratch_shapes=[
                pltpu.VMEM((region, bs, bs), jnp.float32),
                pltpu.VMEM((3 * blocks, region, bs, bs), jnp.float32),
                pltpu.VMEM((ext_rows, 3 * bs, interp_slots * bs), jnp.bfloat16),
            ],
        ),
        compiler_params=pltpu.CompilerParams(dimension_semantics=("arbitrary",)),
    )(table, slot, a_tiles, low, p_tiles, up)

    from_lower = passed_along(to_upper, "tile", 1)
    from_upper = passed_along(to_lower, "tile", -1)

    c_slab = c_cols // (tiles * blocks)
    c_tile = (c_cols // blocks) % tiles
    c_w = c_cols % blocks
    c_ds = (c_slab - s + 1) % slabs - 1
    c_dt = (c_tile - t + 2) % tiles - 2
    base = (c_ds + 1) * 3
    r_idx = jnp.arange(blocks, dtype=jnp.int32)[:, None]

    def pick(part, dt):
        valid = (dt >= -1) & (dt <= 1)
        idx = jnp.clip((base + dt + 1) * blocks + c_w, 0, region - 1)
        tiles_picked = part[r_idx, idx]
        return jnp.where(valid[:, :, None, None], tiles_picked, 0.0)

    early = lax.optimization_barrier(pick(own_part, c_dt) + pick(from_lower, c_dt + 1))
    return early + pick(from_upper, c_dt - 1)


def solution(mesh):
    return jax.shard_map(
        shards,
        mesh=mesh,
        in_specs=(
            P(("slab", "tile"), None, None, None),
            P(("slab", "tile"), None),
            P(("slab", "tile"), None, None, None),
            P(("slab", "tile"), None),
            P(("slab", "tile"), None),
        ),
        out_specs=P(("slab", "tile"), None, None, None),
        check_vma=False,
    )
```

```python
import functools

import jax
import jax.numpy as jnp
from jax import lax
from jax.experimental import pallas as pl
from jax.experimental.pallas import tpu as pltpu
from jax.sharding import PartitionSpec as P

RIM = 4


def passed_along(value, axis, steps):
    count = lax.axis_size(axis)
    pairs = [(source, (source + steps) % count) for source in range(count)]
    return lax.ppermute(value, axis, pairs)


def split(x):
    hi = x.astype(jnp.bfloat16)
    lo = (x - hi.astype(jnp.float32)).astype(jnp.bfloat16)
    return hi, lo


def stack_lhs(x):
    hi, lo = split(x)
    return jnp.concatenate([hi, hi, lo], axis=1)


def stack_rhs(y):
    hi, lo = split(y)
    return jnp.concatenate([hi, lo, hi], axis=0)


def triple_kernel(
    coupling_slots, interp_slots, blocks, region,
    idx_ref, a_ref, low_ref, mid_ref, up_ref, lo_ref, own_ref, hi_ref,
    y_ref, acc_ref, p3_ref,
):
    g = pl.program_id(0)
    steps = pl.num_programs(0)
    per_step = a_ref.shape[0]
    rows = steps * per_step
    bs = a_ref.shape[2]
    slot_base = rows * coupling_slots
    owner_base = slot_base
    rowslot_base = owner_base + rows * interp_slots

    @pl.when(g == 0)
    def _():
        acc_ref[...] = jnp.zeros_like(acc_ref)

        def fill(src, offset, count):
            def body(r, carry):
                for p in range(interp_slots):
                    if len(src.shape) == 2:
                        start = pl.multiple_of((r * interp_slots + p) * bs, bs)
                        tile = src[pl.ds(start, bs), :]
                    else:
                        tile = src[r, p]
                    hi, lo = split(tile)
                    cols = slice(p * bs, (p + 1) * bs)
                    p3_ref[offset + r, 0:bs, cols] = hi
                    p3_ref[offset + r, bs : 2 * bs, cols] = lo
                    p3_ref[offset + r, 2 * bs : 3 * bs, cols] = hi
                return carry

            lax.fori_loop(0, count, body, 0)

        fill(low_ref, 0, RIM)
        fill(mid_ref, RIM, rows)
        fill(up_ref, RIM + rows, RIM)

    def row_step(i, carry):
        gi = g * per_step + i
        y_ref[...] = jnp.zeros_like(y_ref)
        for a in range(coupling_slots):
            row = idx_ref[gi * coupling_slots + a]
            prod = jnp.dot(stack_lhs(a_ref[i, a]), p3_ref[row], preferred_element_type=jnp.float32)
            for p in range(interp_slots):
                slot = idx_ref[rowslot_base + row * interp_slots + p]
                y_ref[slot] += prod[:, p * bs : (p + 1) * bs]
        pt = stack_lhs(jnp.concatenate([mid_ref[gi, q].T for q in range(interp_slots)], axis=0))
        owners = [idx_ref[owner_base + gi * interp_slots + q] for q in range(interp_slots)]
        for c in range(region):
            res = jnp.dot(pt, stack_rhs(y_ref[c]), preferred_element_type=jnp.float32)
            for q in range(interp_slots):
                acc_ref[owners[q], c] += res[q * bs : (q + 1) * bs]
        return carry

    lax.fori_loop(0, per_step, row_step, 0)

    @pl.when(g == steps - 1)
    def _():
        lo_ref[...] = acc_ref[:blocks]
        own_ref[...] = acc_ref[blocks : 2 * blocks]
        hi_ref[...] = acc_ref[2 * blocks :]


def shards(a_tiles, a_cols, p_tiles, p_cols, c_cols):
    rows, coupling_slots, bs, _ = a_tiles.shape
    interp_slots = p_tiles.shape[1]
    blocks, pattern_slots = c_cols.shape
    tiles = lax.axis_size("tile")
    slabs = lax.axis_size("slab")
    t = lax.axis_index("tile")
    s = lax.axis_index("slab")
    device = s * tiles + t
    region = 9 * blocks

    ext_rows = rows + 2 * RIM

    key_count = RIM * interp_slots

    def halo(first):
        keys = p_cols[first : first + RIM].astype(jnp.float32).reshape(1, key_count)
        key_rows = jnp.pad(keys, ((0, 7), (0, bs - key_count)))
        flat = p_tiles[first : first + RIM].reshape(RIM * interp_slots * bs, bs)
        return jnp.concatenate([flat, key_rows], axis=0)

    low = lax.ppermute(halo(rows - RIM), "slab", [(i, i + 1) for i in range(slabs - 1)])
    up = lax.ppermute(halo(0), "slab", [(i + 1, i) for i in range(slabs - 1)])

    def halo_keys(block):
        return block[key_count * bs, :key_count].astype(jnp.int32)

    ext_keys = jnp.concatenate([halo_keys(low), p_cols.reshape(-1), halo_keys(up)])

    own_base = device * rows
    lower_base = (device - tiles) * rows + rows - RIM
    upper_base = (device + tiles) * rows
    local_index = jnp.where(
        a_cols < own_base,
        a_cols - lower_base,
        jnp.where(
            a_cols < own_base + rows,
            RIM + a_cols - own_base,
            RIM + rows + a_cols - upper_base,
        ),
    )
    local_index = jnp.clip(local_index, 0, ext_rows - 1)
    keys = ext_keys
    k_slab = keys // (tiles * blocks)
    k_tile = (keys // blocks) % tiles
    k_dt = (k_tile - t + 1) % tiles - 1
    slot = ((k_slab - s + 1) * 3 + (k_dt + 1)) * blocks + keys % blocks
    slot = jnp.clip(slot, 0, region - 1).astype(jnp.int32)

    targets = p_cols - s * tiles * blocks
    relative = jnp.remainder(targets // blocks - t + 1, tiles)
    owner = jnp.clip(relative * blocks + targets % blocks, 0, 3 * blocks - 1)

    per_step = next(d for d in (2, 1) if rows % d == 0)
    kernel = functools.partial(triple_kernel, coupling_slots, interp_slots, blocks, region)
    part = jax.ShapeDtypeStruct((blocks, region, bs, bs), jnp.float32)
    part_spec = pl.BlockSpec((blocks, region, bs, bs), lambda g, *_: (0, 0, 0, 0))
    table = jnp.concatenate(
        [local_index.reshape(-1), owner.reshape(-1), slot]
    ).astype(jnp.int32)
    to_lower, own_part, to_upper = pl.pallas_call(
        kernel,
        out_shape=(part, part, part),
        grid_spec=pltpu.PrefetchScalarGridSpec(
            num_scalar_prefetch=1,
            grid=(rows // per_step,),
            in_specs=[
                pl.BlockSpec((per_step, coupling_slots, bs, bs), lambda g, *_: (g, 0, 0, 0)),
                pl.BlockSpec(low.shape, lambda g, *_: (0, 0)),
                pl.BlockSpec(p_tiles.shape, lambda g, *_: (0, 0, 0, 0)),
                pl.BlockSpec(up.shape, lambda g, *_: (0, 0)),
            ],
            out_specs=(part_spec, part_spec, part_spec),
            scratch_shapes=[
                pltpu.VMEM((region, bs, bs), jnp.float32),
                pltpu.VMEM((3 * blocks, region, bs, bs), jnp.float32),
                pltpu.VMEM((ext_rows, 3 * bs, interp_slots * bs), jnp.bfloat16),
            ],
        ),
        compiler_params=pltpu.CompilerParams(dimension_semantics=("arbitrary",)),
    )(table, a_tiles, low, p_tiles, up)

    from_lower = passed_along(to_upper, "tile", 1)
    from_upper = passed_along(to_lower, "tile", -1)

    c_slab = c_cols // (tiles * blocks)
    c_tile = (c_cols // blocks) % tiles
    c_w = c_cols % blocks
    c_ds = (c_slab - s + 1) % slabs - 1
    c_dt = (c_tile - t + 2) % tiles - 2
    base = (c_ds + 1) * 3
    r_idx = jnp.arange(blocks, dtype=jnp.int32)[:, None]

    def pick(part, dt):
        valid = (dt >= -1) & (dt <= 1)
        idx = jnp.clip((base + dt + 1) * blocks + c_w, 0, region - 1)
        tiles_picked = part[r_idx, idx]
        return jnp.where(valid[:, :, None, None], tiles_picked, 0.0)

    early = lax.optimization_barrier(pick(own_part, c_dt) + pick(from_lower, c_dt + 1))
    return early + pick(from_upper, c_dt - 1)


def solution(mesh):
    return jax.shard_map(
        shards,
        mesh=mesh,
        in_specs=(
            P(("slab", "tile"), None, None, None),
            P(("slab", "tile"), None),
            P(("slab", "tile"), None, None, None),
            P(("slab", "tile"), None),
            P(("slab", "tile"), None),
        ),
        out_specs=P(("slab", "tile"), None, None, None),
        check_vma=False,
    )
```

```python
import functools

import jax
import jax.numpy as jnp
from jax import lax
from jax.experimental import pallas as pl
from jax.experimental.pallas import tpu as pltpu
from jax.sharding import PartitionSpec as P

RIM = 4


def passed_along(value, axis, steps):
    count = lax.axis_size(axis)
    pairs = [(source, (source + steps) % count) for source in range(count)]
    return lax.ppermute(value, axis, pairs)


def split(x):
    hi = x.astype(jnp.bfloat16)
    lo = (x - hi.astype(jnp.float32)).astype(jnp.bfloat16)
    return hi, lo


def stack_lhs(x):
    hi, lo = split(x)
    return jnp.concatenate([hi, hi, lo], axis=1)


def stack_rhs(y):
    hi, lo = split(y)
    return jnp.concatenate([hi, lo, hi], axis=0)


def triple_kernel(
    coupling_slots, interp_slots, blocks, region,
    idx_ref, a_ref, low_ref, mid_ref, up_ref, lo_ref, own_ref, hi_ref,
    y_ref, acc_ref, p3_ref,
):
    g = pl.program_id(0)
    steps = pl.num_programs(0)
    per_step = a_ref.shape[0]
    rows = steps * per_step
    bs = a_ref.shape[2]
    slot_base = rows * coupling_slots
    owner_base = slot_base
    rowslot_base = owner_base + rows * interp_slots

    @pl.when(g == 0)
    def _():
        acc_ref[...] = jnp.zeros_like(acc_ref)

        def fill(src, offset, count):
            def body(r, carry):
                for p in range(interp_slots):
                    if len(src.shape) == 2:
                        start = pl.multiple_of((r * interp_slots + p) * bs, bs)
                        tile = src[pl.ds(start, bs), :]
                    else:
                        tile = src[r, p]
                    hi, lo = split(tile)
                    cols = slice(p * bs, (p + 1) * bs)
                    p3_ref[offset + r, 0:bs, cols] = hi
                    p3_ref[offset + r, bs : 2 * bs, cols] = lo
                    p3_ref[offset + r, 2 * bs : 3 * bs, cols] = hi
                return carry

            lax.fori_loop(0, count, body, 0)

        fill(low_ref, 0, RIM)
        fill(mid_ref, RIM, rows)
        fill(up_ref, RIM + rows, RIM)

    def row_step(i, carry):
        gi = g * per_step + i
        y_ref[...] = jnp.zeros_like(y_ref)
        for a in range(coupling_slots):
            row = idx_ref[gi * coupling_slots + a]
            prod = jnp.dot(stack_lhs(a_ref[i, a]), p3_ref[row], preferred_element_type=jnp.float32)
            for p in range(interp_slots):
                slot = idx_ref[rowslot_base + row * interp_slots + p]
                y_ref[slot] += prod[:, p * bs : (p + 1) * bs]
        pt = stack_lhs(jnp.concatenate([mid_ref[gi, q].T for q in range(interp_slots)], axis=0))
        owners = [idx_ref[owner_base + gi * interp_slots + q] for q in range(interp_slots)]
        for c in range(region):
            res = jnp.dot(pt, stack_rhs(y_ref[c]), preferred_element_type=jnp.float32)
            for q in range(interp_slots):
                acc_ref[owners[q], c] += res[q * bs : (q + 1) * bs]
        return carry

    lax.fori_loop(0, per_step, row_step, 0)

    @pl.when(g == steps - 1)
    def _():
        lo_ref[...] = acc_ref[:blocks]
        own_ref[...] = acc_ref[blocks : 2 * blocks]
        hi_ref[...] = acc_ref[2 * blocks :]


def shards(a_tiles, a_cols, p_tiles, p_cols, c_cols):
    rows, coupling_slots, bs, _ = a_tiles.shape
    interp_slots = p_tiles.shape[1]
    blocks, pattern_slots = c_cols.shape
    tiles = lax.axis_size("tile")
    slabs = lax.axis_size("slab")
    t = lax.axis_index("tile")
    s = lax.axis_index("slab")
    device = s * tiles + t
    region = 9 * blocks

    ext_rows = rows + 2 * RIM

    key_count = RIM * interp_slots

    def halo(first):
        keys = p_cols[first : first + RIM].astype(jnp.float32).reshape(1, key_count)
        key_rows = jnp.pad(keys, ((0, 7), (0, bs - key_count)))
        flat = p_tiles[first : first + RIM].reshape(RIM * interp_slots * bs, bs)
        return jnp.concatenate([flat, key_rows], axis=0)

    low = lax.ppermute(halo(rows - RIM), "slab", [(i, i + 1) for i in range(slabs - 1)])
    up = lax.ppermute(halo(0), "slab", [(i + 1, i) for i in range(slabs - 1)])

    def halo_keys(block):
        return block[key_count * bs, :key_count].astype(jnp.int32)

    ext_keys = jnp.concatenate([halo_keys(low), p_cols.reshape(-1), halo_keys(up)])

    own_base = device * rows
    lower_base = (device - tiles) * rows + rows - RIM
    upper_base = (device + tiles) * rows
    local_index = jnp.where(
        a_cols < own_base,
        a_cols - lower_base,
        jnp.where(
            a_cols < own_base + rows,
            RIM + a_cols - own_base,
            RIM + rows + a_cols - upper_base,
        ),
    )
    local_index = jnp.clip(local_index, 0, ext_rows - 1)
    keys = ext_keys
    k_slab = keys // (tiles * blocks)
    k_tile = (keys // blocks) % tiles
    k_dt = (k_tile - t + 1) % tiles - 1
    slot = ((k_slab - s + 1) * 3 + (k_dt + 1)) * blocks + keys % blocks
    slot = jnp.clip(slot, 0, region - 1).astype(jnp.int32)

    targets = p_cols - s * tiles * blocks
    relative = jnp.remainder(targets // blocks - t + 1, tiles)
    owner = jnp.clip(relative * blocks + targets % blocks, 0, 3 * blocks - 1)

    per_step = next(d for d in (2, 1) if rows % d == 0)
    kernel = functools.partial(triple_kernel, coupling_slots, interp_slots, blocks, region)
    part = jax.ShapeDtypeStruct((blocks, region, bs, bs), jnp.float32)
    part_spec = pl.BlockSpec((blocks, region, bs, bs), lambda g, *_: (0, 0, 0, 0))
    table = jnp.concatenate(
        [local_index.reshape(-1), owner.reshape(-1), slot]
    ).astype(jnp.int32)
    to_lower, own_part, to_upper = pl.pallas_call(
        kernel,
        out_shape=(part, part, part),
        grid_spec=pltpu.PrefetchScalarGridSpec(
            num_scalar_prefetch=1,
            grid=(rows // per_step,),
            in_specs=[
                pl.BlockSpec((per_step, coupling_slots, bs, bs), lambda g, *_: (g, 0, 0, 0)),
                pl.BlockSpec(low.shape, lambda g, *_: (0, 0)),
                pl.BlockSpec(p_tiles.shape, lambda g, *_: (0, 0, 0, 0)),
                pl.BlockSpec(up.shape, lambda g, *_: (0, 0)),
            ],
            out_specs=(part_spec, part_spec, part_spec),
            scratch_shapes=[
                pltpu.VMEM((region, bs, bs), jnp.float32),
                pltpu.VMEM((3 * blocks, region, bs, bs), jnp.float32),
                pltpu.VMEM((ext_rows, 3 * bs, interp_slots * bs), jnp.bfloat16),
            ],
        ),
        compiler_params=pltpu.CompilerParams(dimension_semantics=("arbitrary",)),
    )(table, a_tiles, low, p_tiles, up)

    from_lower = passed_along(to_upper, "tile", 1)
    from_upper = passed_along(to_lower, "tile", -1)
    c_cols, from_lower = lax.optimization_barrier((c_cols, from_lower))

    c_slab = c_cols // (tiles * blocks)
    c_tile = (c_cols // blocks) % tiles
    c_w = c_cols % blocks
    c_ds = (c_slab - s + 1) % slabs - 1
    c_dt = (c_tile - t + 2) % tiles - 2
    base = (c_ds + 1) * 3
    r_idx = jnp.arange(blocks, dtype=jnp.int32)[:, None]

    def pick(part, dt):
        valid = (dt >= -1) & (dt <= 1)
        idx = jnp.clip((base + dt + 1) * blocks + c_w, 0, region - 1)
        tiles_picked = part[r_idx, idx]
        return jnp.where(valid[:, :, None, None], tiles_picked, 0.0)

    early = lax.optimization_barrier(pick(own_part, c_dt) + pick(from_lower, c_dt + 1))
    return early + pick(from_upper, c_dt - 1)


def solution(mesh):
    return jax.shard_map(
        shards,
        mesh=mesh,
        in_specs=(
            P(("slab", "tile"), None, None, None),
            P(("slab", "tile"), None),
            P(("slab", "tile"), None, None, None),
            P(("slab", "tile"), None),
            P(("slab", "tile"), None),
        ),
        out_specs=P(("slab", "tile"), None, None, None),
        check_vma=False,
    )
```

```python
import functools

import jax
import jax.numpy as jnp
from jax import lax
from jax.experimental import pallas as pl
from jax.experimental.pallas import tpu as pltpu
from jax.sharding import PartitionSpec as P

RIM = 4


def passed_along(value, axis, steps):
    count = lax.axis_size(axis)
    pairs = [(source, (source + steps) % count) for source in range(count)]
    return lax.ppermute(value, axis, pairs)


def split(x):
    hi = x.astype(jnp.bfloat16)
    lo = (x - hi.astype(jnp.float32)).astype(jnp.bfloat16)
    return hi, lo


def stack_lhs(x):
    hi, lo = split(x)
    return jnp.concatenate([hi, hi, lo], axis=1)


def stack_rhs(y):
    hi, lo = split(y)
    return jnp.concatenate([hi, lo, hi], axis=0)


def triple_kernel(
    coupling_slots, interp_slots, blocks, region,
    idx_ref, a_ref, low_ref, mid_ref, up_ref, lo_ref, own_ref, hi_ref,
    y_ref, acc_ref, p3_ref,
):
    g = pl.program_id(0)
    steps = pl.num_programs(0)
    per_step = a_ref.shape[0]
    rows = steps * per_step
    bs = a_ref.shape[2]
    slot_base = rows * coupling_slots
    owner_base = slot_base
    rowslot_base = owner_base + rows * interp_slots

    @pl.when(g == 0)
    def _():
        acc_ref[...] = jnp.zeros_like(acc_ref)

        def fill(src, offset, count):
            def body(r, carry):
                for p in range(interp_slots):
                    if len(src.shape) == 2:
                        start = pl.multiple_of((r * interp_slots + p) * bs, bs)
                        tile = src[pl.ds(start, bs), :]
                    else:
                        tile = src[r, p]
                    hi, lo = split(tile)
                    cols = slice(p * bs, (p + 1) * bs)
                    p3_ref[offset + r, 0:bs, cols] = hi
                    p3_ref[offset + r, bs : 2 * bs, cols] = lo
                    p3_ref[offset + r, 2 * bs : 3 * bs, cols] = hi
                return carry

            lax.fori_loop(0, count, body, 0)

        fill(low_ref, 0, RIM)
        fill(mid_ref, RIM, rows)
        fill(up_ref, RIM + rows, RIM)

    def row_step(i, carry):
        gi = g * per_step + i
        y_ref[...] = jnp.zeros_like(y_ref)
        for a in range(coupling_slots):
            row = idx_ref[gi * coupling_slots + a]
            prod = jnp.dot(stack_lhs(a_ref[i, a]), p3_ref[row], preferred_element_type=jnp.float32)
            for p in range(interp_slots):
                slot = idx_ref[rowslot_base + row * interp_slots + p]
                y_ref[slot] += prod[:, p * bs : (p + 1) * bs]
        pt = stack_lhs(jnp.concatenate([mid_ref[gi, q].T for q in range(interp_slots)], axis=0))
        owners = [idx_ref[owner_base + gi * interp_slots + q] for q in range(interp_slots)]
        for c in range(region):
            res = jnp.dot(pt, stack_rhs(y_ref[c]), preferred_element_type=jnp.float32)
            for q in range(interp_slots):
                acc_ref[owners[q], c] += res[q * bs : (q + 1) * bs]
        return carry

    lax.fori_loop(0, per_step, row_step, 0)

    @pl.when(g == steps - 1)
    def _():
        lo_ref[...] = acc_ref[:blocks]
        own_ref[...] = acc_ref[blocks : 2 * blocks]
        hi_ref[...] = acc_ref[2 * blocks :]


def shards(a_tiles, a_cols, p_tiles, p_cols, c_cols):
    rows, coupling_slots, bs, _ = a_tiles.shape
    interp_slots = p_tiles.shape[1]
    blocks, pattern_slots = c_cols.shape
    tiles = lax.axis_size("tile")
    slabs = lax.axis_size("slab")
    t = lax.axis_index("tile")
    s = lax.axis_index("slab")
    device = s * tiles + t
    region = 9 * blocks

    ext_rows = rows + 2 * RIM

    key_count = RIM * interp_slots

    def halo(first):
        keys = p_cols[first : first + RIM].astype(jnp.float32).reshape(1, key_count)
        key_rows = jnp.pad(keys, ((0, 7), (0, bs - key_count)))
        flat = p_tiles[first : first + RIM].reshape(RIM * interp_slots * bs, bs)
        return jnp.concatenate([flat, key_rows], axis=0)

    low = lax.ppermute(halo(rows - RIM), "slab", [(i, i + 1) for i in range(slabs - 1)])
    up = lax.ppermute(halo(0), "slab", [(i + 1, i) for i in range(slabs - 1)])

    def halo_keys(block):
        return block[key_count * bs, :key_count].astype(jnp.int32)

    ext_keys = jnp.concatenate([halo_keys(low), p_cols.reshape(-1), halo_keys(up)])

    own_base = device * rows
    lower_base = (device - tiles) * rows + rows - RIM
    upper_base = (device + tiles) * rows
    local_index = jnp.where(
        a_cols < own_base,
        a_cols - lower_base,
        jnp.where(
            a_cols < own_base + rows,
            RIM + a_cols - own_base,
            RIM + rows + a_cols - upper_base,
        ),
    )
    local_index = jnp.clip(local_index, 0, ext_rows - 1)
    keys = ext_keys
    k_slab = keys // (tiles * blocks)
    k_tile = (keys // blocks) % tiles
    k_dt = (k_tile - t + 1) % tiles - 1
    slot = ((k_slab - s + 1) * 3 + (k_dt + 1)) * blocks + keys % blocks
    slot = jnp.clip(slot, 0, region - 1).astype(jnp.int32)

    targets = p_cols - s * tiles * blocks
    relative = jnp.remainder(targets // blocks - t + 1, tiles)
    owner = jnp.clip(relative * blocks + targets % blocks, 0, 3 * blocks - 1)

    per_step = 1
    kernel = functools.partial(triple_kernel, coupling_slots, interp_slots, blocks, region)
    part = jax.ShapeDtypeStruct((blocks, region, bs, bs), jnp.float32)
    part_spec = pl.BlockSpec((blocks, region, bs, bs), lambda g, *_: (0, 0, 0, 0))
    table = jnp.concatenate(
        [local_index.reshape(-1), owner.reshape(-1), slot]
    ).astype(jnp.int32)
    to_lower, own_part, to_upper = pl.pallas_call(
        kernel,
        out_shape=(part, part, part),
        grid_spec=pltpu.PrefetchScalarGridSpec(
            num_scalar_prefetch=1,
            grid=(rows // per_step,),
            in_specs=[
                pl.BlockSpec((per_step, coupling_slots, bs, bs), lambda g, *_: (g, 0, 0, 0)),
                pl.BlockSpec(low.shape, lambda g, *_: (0, 0)),
                pl.BlockSpec(p_tiles.shape, lambda g, *_: (0, 0, 0, 0)),
                pl.BlockSpec(up.shape, lambda g, *_: (0, 0)),
            ],
            out_specs=(part_spec, part_spec, part_spec),
            scratch_shapes=[
                pltpu.VMEM((region, bs, bs), jnp.float32),
                pltpu.VMEM((3 * blocks, region, bs, bs), jnp.float32),
                pltpu.VMEM((ext_rows, 3 * bs, interp_slots * bs), jnp.bfloat16),
            ],
        ),
        compiler_params=pltpu.CompilerParams(dimension_semantics=("arbitrary",)),
    )(table, a_tiles, low, p_tiles, up)

    from_lower = passed_along(to_upper, "tile", 1)
    from_upper = passed_along(to_lower, "tile", -1)

    c_slab = c_cols // (tiles * blocks)
    c_tile = (c_cols // blocks) % tiles
    c_w = c_cols % blocks
    c_ds = (c_slab - s + 1) % slabs - 1
    c_dt = (c_tile - t + 2) % tiles - 2
    base = (c_ds + 1) * 3
    r_idx = jnp.arange(blocks, dtype=jnp.int32)[:, None]

    def pick(part, dt):
        valid = (dt >= -1) & (dt <= 1)
        idx = jnp.clip((base + dt + 1) * blocks + c_w, 0, region - 1)
        tiles_picked = part[r_idx, idx]
        return jnp.where(valid[:, :, None, None], tiles_picked, 0.0)

    early = lax.optimization_barrier(pick(own_part, c_dt) + pick(from_lower, c_dt + 1))
    return early + pick(from_upper, c_dt - 1)


def solution(mesh):
    return jax.shard_map(
        shards,
        mesh=mesh,
        in_specs=(
            P(("slab", "tile"), None, None, None),
            P(("slab", "tile"), None),
            P(("slab", "tile"), None, None, None),
            P(("slab", "tile"), None),
            P(("slab", "tile"), None),
        ),
        out_specs=P(("slab", "tile"), None, None, None),
        check_vma=False,
    )
```

```python
import functools

import jax
import jax.numpy as jnp
from jax import lax
from jax.experimental import pallas as pl
from jax.experimental.pallas import tpu as pltpu
from jax.sharding import PartitionSpec as P

RIM = 4


def passed_along(value, axis, steps):
    count = lax.axis_size(axis)
    pairs = [(source, (source + steps) % count) for source in range(count)]
    return lax.ppermute(value, axis, pairs)


def split(x):
    hi = x.astype(jnp.bfloat16)
    lo = (x - hi.astype(jnp.float32)).astype(jnp.bfloat16)
    return hi, lo


def stack_lhs(x):
    hi, lo = split(x)
    return jnp.concatenate([hi, hi, lo], axis=1)


def stack_rhs(y):
    hi, lo = split(y)
    return jnp.concatenate([hi, lo, hi], axis=0)


def triple_kernel(
    coupling_slots, interp_slots, blocks, region,
    idx_ref, a_ref, low_ref, mid_ref, up_ref, lo_ref, own_ref, hi_ref,
    y_ref, acc_ref, p3_ref,
):
    g = pl.program_id(0)
    steps = pl.num_programs(0)
    per_step = a_ref.shape[0]
    rows = steps * per_step
    bs = a_ref.shape[2]
    slot_base = rows * coupling_slots
    owner_base = slot_base
    rowslot_base = owner_base + rows * interp_slots

    @pl.when(g == 0)
    def _():
        acc_ref[...] = jnp.zeros_like(acc_ref)

        def fill(src, offset, count):
            def body(r, carry):
                for p in range(interp_slots):
                    if len(src.shape) == 2:
                        start = pl.multiple_of((r * interp_slots + p) * bs, bs)
                        tile = src[pl.ds(start, bs), :]
                    else:
                        tile = src[r, p]
                    hi, lo = split(tile)
                    cols = slice(p * bs, (p + 1) * bs)
                    p3_ref[offset + r, 0:bs, cols] = hi
                    p3_ref[offset + r, bs : 2 * bs, cols] = lo
                    p3_ref[offset + r, 2 * bs : 3 * bs, cols] = hi
                return carry

            lax.fori_loop(0, count, body, 0)

        fill(low_ref, 0, RIM)
        fill(mid_ref, RIM, rows)
        fill(up_ref, RIM + rows, RIM)

    def row_step(i, carry):
        gi = g * per_step + i
        y_ref[...] = jnp.zeros_like(y_ref)
        for a in range(coupling_slots):
            row = idx_ref[gi * coupling_slots + a]
            prod = jnp.dot(stack_lhs(a_ref[i, a]), p3_ref[row], preferred_element_type=jnp.float32)
            for p in range(interp_slots):
                slot = idx_ref[rowslot_base + row * interp_slots + p]
                y_ref[slot] += prod[:, p * bs : (p + 1) * bs]
        pt = stack_lhs(jnp.concatenate([mid_ref[gi, q].T for q in range(interp_slots)], axis=0))
        owners = [idx_ref[owner_base + gi * interp_slots + q] for q in range(interp_slots)]
        for c in range(region):
            res = jnp.dot(pt, stack_rhs(y_ref[c]), preferred_element_type=jnp.float32)
            for q in range(interp_slots):
                acc_ref[owners[q], c] += res[q * bs : (q + 1) * bs]
        return carry

    lax.fori_loop(0, per_step, row_step, 0)

    @pl.when(g == steps - 1)
    def _():
        lo_ref[...] = acc_ref[:blocks]
        own_ref[...] = acc_ref[blocks : 2 * blocks]
        hi_ref[...] = acc_ref[2 * blocks :]


def shards(a_tiles, a_cols, p_tiles, p_cols, c_cols):
    rows, coupling_slots, bs, _ = a_tiles.shape
    interp_slots = p_tiles.shape[1]
    blocks, pattern_slots = c_cols.shape
    tiles = lax.axis_size("tile")
    slabs = lax.axis_size("slab")
    t = lax.axis_index("tile")
    s = lax.axis_index("slab")
    device = s * tiles + t
    region = 9 * blocks

    ext_rows = rows + 2 * RIM

    key_count = RIM * interp_slots

    def halo(first):
        keys = p_cols[first : first + RIM].astype(jnp.float32).reshape(1, key_count)
        key_rows = jnp.pad(keys, ((0, 7), (0, bs - key_count)))
        flat = p_tiles[first : first + RIM].reshape(RIM * interp_slots * bs, bs)
        return jnp.concatenate([flat, key_rows], axis=0)

    low = lax.ppermute(halo(rows - RIM), "slab", [(i, i + 1) for i in range(slabs - 1)])
    up = lax.ppermute(halo(0), "slab", [(i + 1, i) for i in range(slabs - 1)])

    def halo_keys(block):
        return block[key_count * bs, :key_count].astype(jnp.int32)

    ext_keys = jnp.concatenate([halo_keys(low), p_cols.reshape(-1), halo_keys(up)])

    own_base = device * rows
    lower_base = (device - tiles) * rows + rows - RIM
    upper_base = (device + tiles) * rows
    local_index = jnp.where(
        a_cols < own_base,
        a_cols - lower_base,
        jnp.where(
            a_cols < own_base + rows,
            RIM + a_cols - own_base,
            RIM + rows + a_cols - upper_base,
        ),
    )
    local_index = jnp.clip(local_index, 0, ext_rows - 1)
    keys = ext_keys
    k_slab = keys // (tiles * blocks)
    k_tile = (keys // blocks) % tiles
    k_dt = (k_tile - t + 1) % tiles - 1
    slot = ((k_slab - s + 1) * 3 + (k_dt + 1)) * blocks + keys % blocks
    slot = jnp.clip(slot, 0, region - 1).astype(jnp.int32)

    targets = p_cols - s * tiles * blocks
    relative = jnp.remainder(targets // blocks - t + 1, tiles)
    owner = jnp.clip(relative * blocks + targets % blocks, 0, 3 * blocks - 1)

    per_step = next(d for d in (2, 1) if rows % d == 0)
    kernel = functools.partial(triple_kernel, coupling_slots, interp_slots, blocks, region)
    part = jax.ShapeDtypeStruct((blocks, region, bs, bs), jnp.float32)
    part_spec = pl.BlockSpec((blocks, region, bs, bs), lambda g, *_: (0, 0, 0, 0))
    table = jnp.concatenate(
        [local_index.reshape(-1), owner.reshape(-1), slot]
    ).astype(jnp.int32)
    to_lower, own_part, to_upper = pl.pallas_call(
        kernel,
        out_shape=(part, part, part),
        grid_spec=pltpu.PrefetchScalarGridSpec(
            num_scalar_prefetch=1,
            grid=(rows // per_step,),
            in_specs=[
                pl.BlockSpec((per_step, coupling_slots, bs, bs), lambda g, *_: (g, 0, 0, 0)),
                pl.BlockSpec(low.shape, lambda g, *_: (0, 0)),
                pl.BlockSpec(p_tiles.shape, lambda g, *_: (0, 0, 0, 0)),
                pl.BlockSpec(up.shape, lambda g, *_: (0, 0)),
            ],
            out_specs=(part_spec, part_spec, part_spec),
            scratch_shapes=[
                pltpu.VMEM((region, bs, bs), jnp.float32),
                pltpu.VMEM((3 * blocks, region, bs, bs), jnp.float32),
                pltpu.VMEM((ext_rows, 3 * bs, interp_slots * bs), jnp.bfloat16),
            ],
        ),
        compiler_params=pltpu.CompilerParams(dimension_semantics=("arbitrary",)),
    )(table, a_tiles, low, p_tiles, up)

    from_lower = passed_along(to_upper, "tile", 1)
    from_upper = passed_along(to_lower, "tile", -1)

    c_slab = c_cols // (tiles * blocks)
    c_tile = (c_cols // blocks) % tiles
    c_w = c_cols % blocks
    c_ds = (c_slab - s + 1) % slabs - 1
    c_dt = (c_tile - t + 2) % tiles - 2
    base = (c_ds + 1) * 3
    r_idx = jnp.arange(blocks, dtype=jnp.int32)[:, None]

    def pick(part, dt):
        valid = (dt >= -1) & (dt <= 1)
        idx = jnp.clip((base + dt + 1) * blocks + c_w, 0, region - 1)
        tiles_picked = part[r_idx, idx]
        return jnp.where(valid[:, :, None, None], tiles_picked, 0.0)

    early = lax.optimization_barrier(pick(own_part, c_dt) + pick(from_lower, c_dt + 1))
    dt_up = c_dt - 1
    up_idx = jnp.where((dt_up >= -1) & (dt_up <= 1), (base + dt_up + 1) * blocks + c_w, -1)
    late = sum(
        jnp.where((up_idx == k)[:, :, None, None], from_upper[:, k : k + 1], 0.0) for k in range(region)
    )
    return early + late


def solution(mesh):
    return jax.shard_map(
        shards,
        mesh=mesh,
        in_specs=(
            P(("slab", "tile"), None, None, None),
            P(("slab", "tile"), None),
            P(("slab", "tile"), None, None, None),
            P(("slab", "tile"), None),
            P(("slab", "tile"), None),
        ),
        out_specs=P(("slab", "tile"), None, None, None),
        check_vma=False,
    )
```
